256 devices in a mesh: seq: 64 (over z, y, core), head: 4 (over x).
Axes of the slice: x: 4, y: 4, z: 8, core: 2. Of those that a mesh axis runs over, the one named last changes fastest.
Arguments:
- query: bfloat16 [40960, 2048], P(('seq', 'head')), may hold values from -5 to 5
- key: bfloat16 [40960, 2048], P(('seq', 'head')), may hold values from -5 to 5
- value: bfloat16 [40960, 2048], P(('seq', 'head')), may hold values from -6 to 6
- grad_out: bfloat16 [40960, 2048], P(('seq', 'head')), may hold values from -6 to 6
- rand_blocks: int32 [640, 3], replicated, may hold values from 0 to 639, as said below
Outputs:
- grad_query: bfloat16 [40960, 2048], P(('seq', 'head'))
- grad_key: bfloat16 [40960, 2048], P(('seq', 'head'))
- grad_value: bfloat16 [40960, 2048], P(('seq', 'head'))
The draws below stay inside these ranges and needn't reach their ends.
Inputs may be any that keep to these rules, and one draw needn't show every extreme that they name: `rand_blocks`: row j lists the 3 random key blocks of query block j. Block b lies on index b // 10 of seq. The blocks of one row lie on 3 different indices. No listed block lies on index 0 or on the index of the query block itself. The query blocks of one index of seq list at most 1 block lying on any one other index.
All inputs are finite; a program needn't handle non-finite values.
Results may differ from the reference program's by a relative error of at most 0.008.
Values may be sent and summed in bfloat16 or wider, within the bound.
No kernel may reach another device: no remote copies, remote signals or barrier semaphores. Data moves between devices by JAX's collectives and lax.ppermute only.
A program may use at most 384 MiB of HBM per device.

```python
import jax
import jax.numpy as jnp
from jax import lax

H = 16
HD = 128
BLOCK = 64
G = 2
R = 3
BPD = 10
NB = 640
S = 40960


def base_values(key):
    return jnp.clip(jax.random.normal(key, (NB, BLOCK, H, HD)), -5.0, 5.0)


def draw_query(key, part):
    values_drawn = base_values(jax.random.fold_in(key, 1))
    return values_drawn.reshape(S, H * HD).astype(jnp.bfloat16)


def draw_key(key, part):
    values_drawn = base_values(jax.random.fold_in(key, 2))
    return values_drawn.reshape(S, H * HD).astype(jnp.bfloat16)


def draw_rand_blocks(key, part):
    seq_count = NB // BPD
    wanted = BPD * R
    devices = jnp.arange(seq_count, dtype=jnp.int32)

    def one_device(device, device_key):
        shuffle_key, within_key = jax.random.split(device_key)
        shuffled = jax.random.permutation(shuffle_key, seq_count).astype(jnp.int32)
        barred = (devices == 0) | (devices == device)
        ranked = jnp.argsort(shuffled + seq_count * barred.astype(jnp.int32)).astype(jnp.int32)
        eligible = seq_count - jnp.sum(barred.astype(jnp.int32))
        owners = ranked[jnp.arange(wanted, dtype=jnp.int32) % eligible]
        within = jax.random.randint(within_key, (wanted,), 0, BPD).astype(jnp.int32)
        return (owners * BPD + within).astype(jnp.int32)
    block_table = jax.vmap(one_device)(devices, jax.random.split(key, seq_count))
    return block_table.reshape(NB, R)


def shard_levels(key, extent, pieces, smallest, high):
    gain, own = 1.0, jax.random.fold_in(key, 6)
    for axis_at, blocks in pieces:
        heights = jnp.exp(jax.random.uniform(jax.random.fold_in(own, axis_at), (blocks,), jnp.float32, smallest / len(pieces), high / len(pieces)))
        gain = gain * jnp.repeat(heights, extent[axis_at] // blocks).reshape([-1 if axis == axis_at else 1 for axis in range(len(extent))])
    return gain


def gaussian(stream_key, dims, deviation, limit, pieces=(), held_as=jnp.bfloat16):
    gain = shard_levels(stream_key, dims, pieces, -0.22, 0.18) if pieces else 1.0
    values = jax.random.normal(stream_key, dims, jnp.float32) * deviation * gain
    return jnp.minimum(jnp.maximum(values, -limit), limit).astype(held_as)


def setup_inputs(seed: int = 0) -> dict:
    splits = jax.random.split(jax.random.key(seed), 6)
    query = draw_query(jax.random.fold_in(splits[5], 71), 0)
    key = draw_key(jax.random.fold_in(splits[5], 71), 0)
    value = gaussian(splits[2], (S, H * HD), 1.0, 6.0, ((0, 256),))
    grad_out = gaussian(splits[3], (S, H * HD), 1.0, 6.0, ((0, 256),))
    rand_blocks = draw_rand_blocks(jax.random.fold_in(splits[5], 71), 0)
    return dict(query=query, key=key, value=value, grad_out=grad_out, rand_blocks=rand_blocks)


big_negative = -1.0e30


def reference(query, key, value, grad_out, rand_blocks):
    score_scale = HD ** -0.5
    query_blocks = query.reshape(NB, BLOCK, H, HD)
    key_blocks = key.reshape(NB, BLOCK, H, HD)
    value_blocks = value.reshape(NB, BLOCK, H, HD)
    dout_blocks = grad_out.reshape(NB, BLOCK, H, HD)

    def visit_block(carry, block_index):
        key_sums, value_sums = carry
        glob_index = jnp.arange(G, dtype=jnp.int32)
        chosen = jnp.concatenate([jnp.stack([block_index - 1, block_index, block_index + 1]).astype(jnp.int32), glob_index, rand_blocks[block_index].astype(jnp.int32)])
        live_slots = jnp.concatenate([jnp.stack([block_index >= 1, block_index >= 0, block_index <= NB - 2]), jnp.abs(glob_index - block_index) > 1, jnp.ones((R,), jnp.bool_)])
        clamped = jnp.clip(chosen, 0, NB - 1).astype(jnp.int32)
        slot_keys = key_blocks[clamped].astype(jnp.float32)
        slot_values = value_blocks[clamped].astype(jnp.float32)
        rows_query = query_blocks[block_index].astype(jnp.float32)
        rows_dout = dout_blocks[block_index].astype(jnp.float32)
        scores = jnp.einsum("xhd,kyhd->hxky", rows_query, slot_keys) * score_scale
        scores = jnp.where(live_slots[None, None, :, None], scores, big_negative)
        row_max = jnp.max(scores, axis=(2, 3), keepdims=True)
        weights = jnp.exp(scores - row_max)
        probabilities = weights / jnp.sum(weights, axis=(2, 3), keepdims=True)
        prob_low = lax.optimization_barrier(probabilities.astype(jnp.bfloat16)).astype(jnp.float32)
        prob_grads = jnp.einsum("xhd,kyhd->hxky", rows_dout, slot_values)
        row_dot = jnp.sum(probabilities * prob_grads, axis=(2, 3), keepdims=True)
        score_grads = lax.optimization_barrier((probabilities * (prob_grads - row_dot)).astype(jnp.bfloat16)).astype(jnp.float32)
        query_grads = jnp.einsum("hxky,kyhd->xhd", score_grads, slot_keys) * score_scale
        key_terms = jnp.einsum("hxky,xhd->kyhd", score_grads, rows_query) * score_scale
        value_terms = jnp.einsum("hxky,xhd->kyhd", prob_low, rows_dout)
        key_sums = key_sums.at[clamped].add(key_terms)
        value_sums = value_sums.at[clamped].add(value_terms)
        return (key_sums, value_sums), query_grads.astype(jnp.bfloat16)

    empty_sums = jnp.zeros((NB, BLOCK, H, HD), jnp.float32)
    (key_sums, value_sums), query_grads = lax.scan(visit_block, (empty_sums, empty_sums), jnp.arange(NB, dtype=jnp.int32))
    return (query_grads.reshape(S, H * HD), key_sums.reshape(S, H * HD).astype(jnp.bfloat16), value_sums.reshape(S, H * HD).astype(jnp.bfloat16))
```

```python
import jax
import jax.numpy as jnp
from jax import lax
from jax.sharding import PartitionSpec as P

HD = 128
BLOCK = 64
G = 2
R = 3


big_negative = -1e30


def broadcast(block, axis, source):
    peers = lax.axis_size(axis)
    block = jnp.where(lax.axis_index(axis) == source, block, jnp.zeros_like(block))
    step = 1
    while step * 2 < peers:
        step *= 2
    while step >= 1:
        pairs = [(i, i + step) for i in range(0, peers, 2 * step) if i + step < peers]
        block = block + lax.ppermute(block, axis, pairs)
        step //= 2
    return block


def reduce_to_first(block, axis):
    peers = lax.axis_size(axis)
    step = 1
    while step < peers:
        pairs = [(i + step, i) for i in range(0, peers, 2 * step) if i + step < peers]
        block = block + lax.ppermute(block, axis, pairs)
        step *= 2
    return block


def extended_2(shard, sides, width):
    for axis, dim in sides:
        peers, length = (lax.axis_size(axis), shard.shape[dim])
        up = [(i, (i + 1) % peers) for i in range(peers - 1)]
        down = [(j, i) for i, j in up]
        last = lax.slice_in_dim(shard, length - width, length, axis=dim)
        leading = lax.slice_in_dim(shard, 0, width, axis=dim)
        before = lax.ppermute(last, axis, up)
        after = lax.ppermute(leading, axis, down)
        shard = jnp.concatenate([before, shard, after], axis=dim)
    return shard


def request_plan(requested, device, per_dev):
    wanted_row = requested[device]
    owners = wanted_row // per_dev
    within = wanted_row % per_dev
    usable = jnp.ones(wanted_row.shape, jnp.bool_)
    positions = jnp.arange(owners.shape[0])
    earlier = (owners[:, None] == owners[None, :]) & (positions[None, :] < positions[:, None])
    slot_rank = jnp.sum(earlier.astype(jnp.int32), axis=1)
    return (owners, within, slot_rank, usable)


def on_device(query, key, value, grad_out, rand_blocks):
    queries, keys, values, out_grads = (
        lax.all_to_all(query, "head", split_axis=1, concat_axis=0, tiled=True),
        lax.all_to_all(key, "head", split_axis=1, concat_axis=0, tiled=True),
        lax.all_to_all(value, "head", split_axis=1, concat_axis=0, tiled=True),
        lax.all_to_all(grad_out, "head", split_axis=1, concat_axis=0, tiled=True),
    )
    tokens, features = queries.shape
    head_count = features // HD
    per_dev = tokens // BLOCK
    seq_count = lax.axis_size("seq")
    device = lax.axis_index("seq")
    capacity = (per_dev * R + seq_count - 3) // (seq_count - 2)
    rand_count = per_dev * R
    slots_total = 3 + G + R
    score_scale = HD ** (-0.5)
    requested = rand_blocks.reshape(seq_count, rand_count)
    owners_all, within_all, rank_all, usable_all = jax.vmap(
        lambda sender: request_plan(requested, sender, per_dev)
    )(jnp.arange(seq_count, dtype=jnp.int32))
    to_me = usable_all & (owners_all == device)
    slot_ids = jnp.arange(capacity)
    block_ids = jnp.arange(per_dev)
    matches = (
        to_me[:, :, None, None]
        & (rank_all[:, :, None, None] == slot_ids[None, None, :, None])
        & (within_all[:, :, None, None] == block_ids[None, None, None, :])
    )
    chooser = jnp.sum(matches.astype(jnp.float32), axis=1)
    my_owners, my_within, my_rank, my_usable = request_plan(requested, device, per_dev)
    my_slot = jnp.clip(my_owners, 0, seq_count - 1) * capacity + my_rank
    own_pairs = jnp.stack([keys, values]).reshape(2, per_dev, BLOCK, features)
    served = None
    served = jnp.einsum(
        "dcb,sbxf->dcsxf",
        chooser.astype(jnp.bfloat16),
        own_pairs,
        preferred_element_type=jnp.float32,
    ).astype(jnp.bfloat16)
    outgoing = served.reshape(seq_count * capacity, 2, BLOCK, features)
    incoming = lax.all_to_all(outgoing, "seq", split_axis=0, concat_axis=0, tiled=True)
    fetched = incoming[my_slot]
    leading = jnp.stack([keys[: G * BLOCK], values[: G * BLOCK]])
    global_pairs = broadcast(leading, "seq", 0).reshape(2, G, BLOCK, features)
    extended = extended_2(jnp.stack([keys, values]), (("seq", 1),), BLOCK)
    left_pair = extended[:, :BLOCK]
    right_pair = extended[:, -BLOCK:]
    framed = jnp.concatenate([left_pair[:, None], own_pairs, right_pair[:, None]], axis=1)
    window = jnp.stack(
        [framed[:, 0:per_dev], framed[:, 1 : per_dev + 1], framed[:, 2 : per_dev + 2]], axis=2
    )
    global_slots = jnp.broadcast_to(global_pairs[:, None], (2, per_dev, G, BLOCK, features))
    randoms = fetched.reshape(per_dev, R, 2, BLOCK, features).transpose(2, 0, 1, 3, 4)
    gathered = jnp.concatenate([window, global_slots, randoms], axis=2)
    slot_keys = gathered[0].reshape(per_dev, slots_total, BLOCK, head_count, HD)
    slot_values = gathered[1].reshape(per_dev, slots_total, BLOCK, head_count, HD)
    block_index = device * per_dev + jnp.arange(per_dev)
    glob_index = jnp.arange(G)
    intersections = jnp.abs(glob_index[None, :] - block_index[:, None]) <= 1
    live_slots = jnp.concatenate(
        [
            (block_index >= 1)[:, None],
            jnp.ones((per_dev, 1), jnp.bool_),
            (block_index <= seq_count * per_dev - 2)[:, None],
            jnp.logical_not(intersections),
            jnp.ones((per_dev, R), jnp.bool_),
        ],
        axis=1,
    )
    query_blocks = queries.reshape(per_dev, BLOCK, head_count, HD)
    dout_blocks = out_grads.reshape(per_dev, BLOCK, head_count, HD)
    scores = (
        jnp.einsum("bxhd,bkyhd->bhxky", query_blocks, slot_keys, preferred_element_type=jnp.float32)
        * score_scale
    )
    scores = jnp.where(live_slots[:, None, None, :, None], scores, big_negative)
    row_max = jnp.max(scores, axis=(3, 4), keepdims=True)
    weights = jnp.exp(scores - row_max)
    row_total = jnp.sum(weights, axis=(3, 4), keepdims=True)
    probabilities = weights / row_total
    prob_low = probabilities.astype(jnp.bfloat16)
    prob_grads = jnp.einsum(
        "bxhd,bkyhd->bhxky", dout_blocks, slot_values, preferred_element_type=jnp.float32
    )
    row_dot = jnp.sum(probabilities * prob_grads, axis=(3, 4), keepdims=True)
    score_grads = (probabilities * (prob_grads - row_dot)).astype(jnp.bfloat16)
    query_grads = (
        jnp.einsum("bhxky,bkyhd->bxhd", score_grads, slot_keys, preferred_element_type=jnp.float32)
        * score_scale
    )
    key_terms = (
        jnp.einsum(
            "bhxky,bxhd->bkyhd", score_grads, query_blocks, preferred_element_type=jnp.float32
        )
        * score_scale
    )
    value_terms = jnp.einsum(
        "bhxky,bxhd->bkyhd", prob_low, dout_blocks, preferred_element_type=jnp.float32
    )
    pair_terms = jnp.stack([key_terms, value_terms]).reshape(
        2, per_dev, slots_total, BLOCK, features
    )
    framed_sum = jnp.pad(pair_terms[:, :, 0], ((0, 0), (0, 2), (0, 0), (0, 0)))
    framed_sum = framed_sum + jnp.pad(pair_terms[:, :, 1], ((0, 0), (1, 1), (0, 0), (0, 0)))
    framed_sum = framed_sum + jnp.pad(pair_terms[:, :, 2], ((0, 0), (2, 0), (0, 0), (0, 0)))
    totals = framed_sum[:, 1 : per_dev + 1]
    global_sum = jnp.sum(pair_terms[:, :, 3 : 3 + G], axis=1)
    rim_terms = jnp.concatenate([framed_sum[:, 0], framed_sum[:, -1]], axis=1)
    widened = extended_2(rim_terms.astype(jnp.bfloat16), (("seq", 1),), BLOCK).astype(
        rim_terms.dtype
    )
    totals = totals.at[:, 0].add(widened[:, :BLOCK])
    totals = totals.at[:, per_dev - 1].add(widened[:, -BLOCK:])
    target = jnp.where(my_usable, my_slot, seq_count * capacity)
    rand_terms = (
        pair_terms[:, :, 3 + G :].reshape(2, rand_count, BLOCK, features).transpose(1, 0, 2, 3)
    )
    outgoing_back = (
        jnp.zeros((seq_count * capacity, 2, BLOCK, features), jnp.float32)
        .at[target]
        .set(rand_terms, mode="drop")
    )
    arrived = lax.all_to_all(
        outgoing_back.astype(jnp.bfloat16), "seq", split_axis=0, concat_axis=0, tiled=True
    ).astype(outgoing_back.dtype)
    collected = jnp.einsum(
        "dcb,dcsxf->sbxf",
        chooser,
        arrived.reshape(seq_count, capacity, 2, BLOCK, features),
        precision=lax.Precision.HIGHEST,
    )
    everywhere = reduce_to_first(global_sum, "seq")
    padded_global = jnp.pad(everywhere, ((0, 0), (0, per_dev - G), (0, 0), (0, 0))) * (
        device == 0
    ).astype(jnp.float32)
    totals = totals + collected + padded_global
    grad_rows = query_grads.reshape(tokens, features).astype(jnp.bfloat16)
    key_rows = totals[0].reshape(tokens, features).astype(jnp.bfloat16)
    value_rows = totals[1].reshape(tokens, features).astype(jnp.bfloat16)
    return (
        lax.all_to_all(grad_rows, "head", split_axis=0, concat_axis=1, tiled=True),
        lax.all_to_all(key_rows, "head", split_axis=0, concat_axis=1, tiled=True),
        lax.all_to_all(value_rows, "head", split_axis=0, concat_axis=1, tiled=True),
    )


def solution(mesh):
    in_specs = (
        P(("seq", "head"), None),
        P(("seq", "head"), None),
        P(("seq", "head"), None),
        P(("seq", "head"), None),
        P(),
    )
    out_specs = (P(("seq", "head"), None), P(("seq", "head"), None), P(("seq", "head"), None))
    return jax.shard_map(
        on_device, mesh=mesh, in_specs=in_specs, out_specs=out_specs, check_vma=False
    )
```

```python
import jax
import jax.numpy as jnp
from jax import lax
from jax.sharding import PartitionSpec as P

HD = 128
BLOCK = 64
G = 2
R = 3


big_negative = -1e30


def broadcast(block, axis, source):
    peers = lax.axis_size(axis)
    block = jnp.where(lax.axis_index(axis) == source, block, jnp.zeros_like(block))
    step = 1
    while step * 2 < peers:
        step *= 2
    while step >= 1:
        pairs = [(i, i + step) for i in range(0, peers, 2 * step) if i + step < peers]
        block = block + lax.ppermute(block, axis, pairs)
        step //= 2
    return block


def reduce_to_first(block, axis):
    peers = lax.axis_size(axis)
    step = 1
    while step < peers:
        pairs = [(i + step, i) for i in range(0, peers, 2 * step) if i + step < peers]
        block = block + lax.ppermute(block, axis, pairs)
        step *= 2
    return block


def extended_2(shard, sides, width):
    for axis, dim in sides:
        peers, length = (lax.axis_size(axis), shard.shape[dim])
        up = [(i, (i + 1) % peers) for i in range(peers - 1)]
        down = [(j, i) for i, j in up]
        last = lax.slice_in_dim(shard, length - width, length, axis=dim)
        leading = lax.slice_in_dim(shard, 0, width, axis=dim)
        before = lax.ppermute(last, axis, up)
        after = lax.ppermute(leading, axis, down)
        shard = jnp.concatenate([before, shard, after], axis=dim)
    return shard


def request_plan(requested, device, per_dev):
    wanted_row = requested[device]
    owners = wanted_row // per_dev
    within = wanted_row % per_dev
    usable = jnp.ones(wanted_row.shape, jnp.bool_)
    positions = jnp.arange(owners.shape[0])
    earlier = (owners[:, None] == owners[None, :]) & (positions[None, :] < positions[:, None])
    slot_rank = jnp.sum(earlier.astype(jnp.int32), axis=1)
    return (owners, within, slot_rank, usable)


def on_device(query, key, value, grad_out, rand_blocks):
    stacked = jnp.stack([query, key, value, grad_out])
    stacked = lax.all_to_all(stacked, "head", split_axis=2, concat_axis=1, tiled=True)
    queries, keys, values, out_grads = stacked[0], stacked[1], stacked[2], stacked[3]
    tokens, features = queries.shape
    head_count = features // HD
    per_dev = tokens // BLOCK
    seq_count = lax.axis_size("seq")
    device = lax.axis_index("seq")
    capacity = (per_dev * R + seq_count - 3) // (seq_count - 2)
    rand_count = per_dev * R
    score_scale = HD ** (-0.5)
    requested = rand_blocks.reshape(seq_count, rand_count)
    owners_all, within_all, rank_all, usable_all = jax.vmap(
        lambda sender: request_plan(requested, sender, per_dev)
    )(jnp.arange(seq_count, dtype=jnp.int32))
    to_me = usable_all & (owners_all == device)
    slot_ids = jnp.arange(capacity)
    block_ids = jnp.arange(per_dev)
    matches = (
        to_me[:, :, None, None]
        & (rank_all[:, :, None, None] == slot_ids[None, None, :, None])
        & (within_all[:, :, None, None] == block_ids[None, None, None, :])
    )
    chooser = jnp.sum(matches.astype(jnp.float32), axis=1)
    my_owners, my_within, my_rank, my_usable = request_plan(requested, device, per_dev)
    my_slot = jnp.clip(my_owners, 0, seq_count - 1) * capacity + my_rank
    own_pairs = jnp.stack([keys, values]).reshape(2, per_dev, BLOCK, features)
    served = jnp.einsum(
        "dcb,sbxf->dcsxf",
        chooser.astype(jnp.bfloat16),
        own_pairs,
        preferred_element_type=jnp.float32,
    ).astype(jnp.bfloat16)
    outgoing = served.reshape(seq_count * capacity, 2, BLOCK, features)
    leading = jnp.stack([keys[: G * BLOCK], values[: G * BLOCK]])
    global_pairs = broadcast(leading, "seq", 0).reshape(2, G, BLOCK, features)
    extended = extended_2(jnp.stack([keys, values]), (("seq", 1),), BLOCK)
    outgoing, global_pairs, extended = lax.optimization_barrier((outgoing, global_pairs, extended))
    incoming = lax.all_to_all(outgoing, "seq", split_axis=0, concat_axis=0, tiled=True)

    left_pair = extended[:, :BLOCK]
    right_pair = extended[:, -BLOCK:]
    framed = jnp.concatenate([left_pair[:, None], own_pairs, right_pair[:, None]], axis=1)
    window = jnp.stack(
        [framed[:, 0:per_dev], framed[:, 1 : per_dev + 1], framed[:, 2 : per_dev + 2]], axis=2
    )
    global_slots = jnp.broadcast_to(global_pairs[:, None], (2, per_dev, G, BLOCK, features))
    local = jnp.concatenate([window, global_slots], axis=2)
    local_count = 3 + G
    local_keys = local[0].reshape(per_dev, local_count, BLOCK, head_count, HD)
    local_values = local[1].reshape(per_dev, local_count, BLOCK, head_count, HD)
    block_index = device * per_dev + jnp.arange(per_dev)
    glob_index = jnp.arange(G)
    intersections = jnp.abs(glob_index[None, :] - block_index[:, None]) <= 1
    live_local = jnp.concatenate(
        [
            (block_index >= 1)[:, None],
            jnp.ones((per_dev, 1), jnp.bool_),
            (block_index <= seq_count * per_dev - 2)[:, None],
            jnp.logical_not(intersections),
        ],
        axis=1,
    )
    query_blocks = queries.reshape(per_dev, BLOCK, head_count, HD)
    dout_blocks = out_grads.reshape(per_dev, BLOCK, head_count, HD)
    scores_local = (
        jnp.einsum("bxhd,bkyhd->bhxky", query_blocks, local_keys, preferred_element_type=jnp.float32)
        * score_scale
    )
    scores_local = jnp.where(live_local[:, None, None, :, None], scores_local, big_negative)
    grads_local = jnp.einsum(
        "bxhd,bkyhd->bhxky", dout_blocks, local_values, preferred_element_type=jnp.float32
    )
    max_local = jnp.max(scores_local, axis=(3, 4), keepdims=True)

    fetched = incoming[my_slot]
    randoms = fetched.reshape(per_dev, R, 2, BLOCK, features)
    rand_keys = randoms[:, :, 0].reshape(per_dev, R, BLOCK, head_count, HD)
    rand_values = randoms[:, :, 1].reshape(per_dev, R, BLOCK, head_count, HD)
    scores_rand = (
        jnp.einsum("bxhd,bkyhd->bhxky", query_blocks, rand_keys, preferred_element_type=jnp.float32)
        * score_scale
    )
    grads_rand = jnp.einsum(
        "bxhd,bkyhd->bhxky", dout_blocks, rand_values, preferred_element_type=jnp.float32
    )
    row_max = jnp.maximum(max_local, jnp.max(scores_rand, axis=(3, 4), keepdims=True))
    weights_local = jnp.exp(scores_local - row_max)
    weights_rand = jnp.exp(scores_rand - row_max)
    row_total = jnp.sum(weights_local, axis=(3, 4), keepdims=True) + jnp.sum(
        weights_rand, axis=(3, 4), keepdims=True
    )
    probs_local = weights_local / row_total
    probs_rand = weights_rand / row_total
    row_dot = jnp.sum(probs_local * grads_local, axis=(3, 4), keepdims=True) + jnp.sum(
        probs_rand * grads_rand, axis=(3, 4), keepdims=True
    )
    dscores_rand = (probs_rand * (grads_rand - row_dot)).astype(jnp.bfloat16)
    low_rand = probs_rand.astype(jnp.bfloat16)
    key_rand = (
        jnp.einsum(
            "bhxky,bxhd->bkyhd", dscores_rand, query_blocks, preferred_element_type=jnp.float32
        )
        * score_scale
    )
    value_rand = jnp.einsum(
        "bhxky,bxhd->bkyhd", low_rand, dout_blocks, preferred_element_type=jnp.float32
    )
    rand_terms = (
        jnp.stack([key_rand, value_rand])
        .reshape(2, rand_count, BLOCK, features)
        .transpose(1, 0, 2, 3)
        .astype(jnp.bfloat16)
    )
    target = jnp.where(my_usable, my_slot, seq_count * capacity)
    placer = (target[:, None] == jnp.arange(seq_count * capacity)[None, :]).astype(jnp.bfloat16)
    outgoing_back = jnp.einsum(
        "js,jkxf->skxf", placer, rand_terms, preferred_element_type=jnp.float32
    ).astype(jnp.bfloat16)
    arrived = lax.all_to_all(outgoing_back, "seq", split_axis=0, concat_axis=0, tiled=True)

    dscores_local = (probs_local * (grads_local - row_dot)).astype(jnp.bfloat16)
    low_local = probs_local.astype(jnp.bfloat16)
    query_grads = (
        jnp.einsum(
            "bhxky,bkyhd->bxhd", dscores_local, local_keys, preferred_element_type=jnp.float32
        )
        + jnp.einsum(
            "bhxky,bkyhd->bxhd", dscores_rand, rand_keys, preferred_element_type=jnp.float32
        )
    ) * score_scale
    key_terms = (
        jnp.einsum(
            "bhxky,bxhd->bkyhd", dscores_local, query_blocks, preferred_element_type=jnp.float32
        )
        * score_scale
    )
    value_terms = jnp.einsum(
        "bhxky,bxhd->bkyhd", low_local, dout_blocks, preferred_element_type=jnp.float32
    )
    pair_terms = jnp.stack([key_terms, value_terms]).reshape(
        2, per_dev, local_count, BLOCK, features
    )
    framed_sum = jnp.pad(pair_terms[:, :, 0], ((0, 0), (0, 2), (0, 0), (0, 0)))
    framed_sum = framed_sum + jnp.pad(pair_terms[:, :, 1], ((0, 0), (1, 1), (0, 0), (0, 0)))
    framed_sum = framed_sum + jnp.pad(pair_terms[:, :, 2], ((0, 0), (2, 0), (0, 0), (0, 0)))
    totals = framed_sum[:, 1 : per_dev + 1]
    global_sum = jnp.sum(pair_terms[:, :, 3 : 3 + G], axis=1)
    rim_terms = jnp.concatenate([framed_sum[:, 0], framed_sum[:, -1]], axis=1)
    widened = extended_2(rim_terms.astype(jnp.bfloat16), (("seq", 1),), BLOCK).astype(
        rim_terms.dtype
    )
    totals = totals.at[:, 0].add(widened[:, :BLOCK])
    totals = totals.at[:, per_dev - 1].add(widened[:, -BLOCK:])
    everywhere = reduce_to_first(global_sum, "seq")
    padded_global = jnp.pad(everywhere, ((0, 0), (0, per_dev - G), (0, 0), (0, 0))) * (
        device == 0
    ).astype(jnp.float32)
    totals = totals + padded_global
    collected = jnp.einsum(
        "dcb,dcsxf->sbxf",
        chooser.astype(jnp.bfloat16),
        arrived.reshape(seq_count, capacity, 2, BLOCK, features),
        preferred_element_type=jnp.float32,
    )
    totals = totals + collected
    grad_rows = query_grads.reshape(tokens, features).astype(jnp.bfloat16)
    key_rows = totals[0].reshape(tokens, features).astype(jnp.bfloat16)
    value_rows = totals[1].reshape(tokens, features).astype(jnp.bfloat16)
    result = jnp.stack([grad_rows, key_rows, value_rows])
    result = lax.all_to_all(result, "head", split_axis=1, concat_axis=2, tiled=True)
    return (result[0], result[1], result[2])


def solution(mesh):
    in_specs = (
        P(("seq", "head"), None),
        P(("seq", "head"), None),
        P(("seq", "head"), None),
        P(("seq", "head"), None),
        P(),
    )
    out_specs = (P(("seq", "head"), None), P(("seq", "head"), None), P(("seq", "head"), None))
    return jax.shard_map(
        on_device, mesh=mesh, in_specs=in_specs, out_specs=out_specs, check_vma=False
    )
```

```python
import jax
import jax.numpy as jnp
from jax import lax
from jax.sharding import PartitionSpec as P

HD = 128
BLOCK = 64
G = 2
R = 3


big_negative = -1e30


def broadcast(block, axis, source):
    peers = lax.axis_size(axis)
    block = jnp.where(lax.axis_index(axis) == source, block, jnp.zeros_like(block))
    inner = 8 if peers % 8 == 0 else 1
    if inner > 1 and source == 0:
        outer = peers // inner
        received = [
            lax.ppermute(block, axis, [(0, k * inner)]) for k in range(1, outer)
        ]
        for part in received:
            block = block + part
        received = [
            lax.ppermute(block, axis, [(z * inner, z * inner + k) for z in range(outer)])
            for k in range(1, inner)
        ]
        for part in received:
            block = block + part
        return block
    step = 1
    while step * 2 < peers:
        step *= 2
    while step >= 1:
        pairs = [(i, i + step) for i in range(0, peers, 2 * step) if i + step < peers]
        block = block + lax.ppermute(block, axis, pairs)
        step //= 2
    return block


def reduce_to_first(block, axis):
    peers = lax.axis_size(axis)
    step = 1
    while step < peers:
        pairs = [(i + step, i) for i in range(0, peers, 2 * step) if i + step < peers]
        block = block + lax.ppermute(block, axis, pairs)
        step *= 2
    return block


def extended_2(shard, sides, width):
    for axis, dim in sides:
        peers, length = (lax.axis_size(axis), shard.shape[dim])
        up = [(i, (i + 1) % peers) for i in range(peers - 1)]
        down = [(j, i) for i, j in up]
        last = lax.slice_in_dim(shard, length - width, length, axis=dim)
        leading = lax.slice_in_dim(shard, 0, width, axis=dim)
        before = lax.ppermute(last, axis, up)
        after = lax.ppermute(leading, axis, down)
        shard = jnp.concatenate([before, shard, after], axis=dim)
    return shard


def request_plan(requested, device, per_dev):
    wanted_row = requested[device]
    owners = wanted_row // per_dev
    within = wanted_row % per_dev
    usable = jnp.ones(wanted_row.shape, jnp.bool_)
    positions = jnp.arange(owners.shape[0])
    earlier = (owners[:, None] == owners[None, :]) & (positions[None, :] < positions[:, None])
    slot_rank = jnp.sum(earlier.astype(jnp.int32), axis=1)
    return (owners, within, slot_rank, usable)


def attend_chunk(queries, out_grads, own_pairs, outgoing, global_pairs, extended,
                 chooser, my_slot, my_usable, device, seq_count, capacity):
    tokens, features = queries.shape
    head_count = features // HD
    per_dev = tokens // BLOCK
    rand_count = per_dev * R
    score_scale = HD ** (-0.5)
    incoming = lax.all_to_all(outgoing, "seq", split_axis=0, concat_axis=0, tiled=True)

    left_pair = extended[:, :BLOCK]
    right_pair = extended[:, -BLOCK:]
    framed = jnp.concatenate([left_pair[:, None], own_pairs, right_pair[:, None]], axis=1)
    window = jnp.stack(
        [framed[:, 0:per_dev], framed[:, 1 : per_dev + 1], framed[:, 2 : per_dev + 2]], axis=2
    )
    global_slots = jnp.broadcast_to(global_pairs[:, None], (2, per_dev, G, BLOCK, features))
    local = jnp.concatenate([window, global_slots], axis=2)
    local_count = 3 + G
    local_keys = local[0].reshape(per_dev, local_count, BLOCK, head_count, HD)
    local_values = local[1].reshape(per_dev, local_count, BLOCK, head_count, HD)
    block_index = device * per_dev + jnp.arange(per_dev)
    glob_index = jnp.arange(G)
    intersections = jnp.abs(glob_index[None, :] - block_index[:, None]) <= 1
    live_local = jnp.concatenate(
        [
            (block_index >= 1)[:, None],
            jnp.ones((per_dev, 1), jnp.bool_),
            (block_index <= seq_count * per_dev - 2)[:, None],
            jnp.logical_not(intersections),
        ],
        axis=1,
    )
    query_blocks = queries.reshape(per_dev, BLOCK, head_count, HD)
    dout_blocks = out_grads.reshape(per_dev, BLOCK, head_count, HD)
    scores_local = (
        jnp.einsum("bxhd,bkyhd->bhxky", query_blocks, local_keys, preferred_element_type=jnp.float32)
        * score_scale
    )
    scores_local = jnp.where(live_local[:, None, None, :, None], scores_local, big_negative)
    grads_local = jnp.einsum(
        "bxhd,bkyhd->bhxky", dout_blocks, local_values, preferred_element_type=jnp.float32
    )
    max_local = jnp.max(scores_local, axis=(3, 4), keepdims=True)

    fetched = incoming[my_slot]
    randoms = fetched.reshape(per_dev, R, 2, BLOCK, features)
    rand_keys = randoms[:, :, 0].reshape(per_dev, R, BLOCK, head_count, HD)
    rand_values = randoms[:, :, 1].reshape(per_dev, R, BLOCK, head_count, HD)
    scores_rand = (
        jnp.einsum("bxhd,bkyhd->bhxky", query_blocks, rand_keys, preferred_element_type=jnp.float32)
        * score_scale
    )
    grads_rand = jnp.einsum(
        "bxhd,bkyhd->bhxky", dout_blocks, rand_values, preferred_element_type=jnp.float32
    )
    row_max = jnp.maximum(max_local, jnp.max(scores_rand, axis=(3, 4), keepdims=True))
    weights_local = jnp.exp(scores_local - row_max)
    weights_rand = jnp.exp(scores_rand - row_max)
    row_total = jnp.sum(weights_local, axis=(3, 4), keepdims=True) + jnp.sum(
        weights_rand, axis=(3, 4), keepdims=True
    )
    probs_local = weights_local / row_total
    probs_rand = weights_rand / row_total
    row_dot = jnp.sum(probs_local * grads_local, axis=(3, 4), keepdims=True) + jnp.sum(
        probs_rand * grads_rand, axis=(3, 4), keepdims=True
    )
    dscores_rand = (probs_rand * (grads_rand - row_dot)).astype(jnp.bfloat16)
    low_rand = probs_rand.astype(jnp.bfloat16)
    key_rand = (
        jnp.einsum(
            "bhxky,bxhd->bkyhd", dscores_rand, query_blocks, preferred_element_type=jnp.float32
        )
        * score_scale
    )
    value_rand = jnp.einsum(
        "bhxky,bxhd->bkyhd", low_rand, dout_blocks, preferred_element_type=jnp.float32
    )
    rand_terms = (
        jnp.stack([key_rand, value_rand])
        .reshape(2, rand_count, BLOCK, features)
        .transpose(1, 0, 2, 3)
        .astype(jnp.bfloat16)
    )
    target = jnp.where(my_usable, my_slot, seq_count * capacity)
    placer = (target[:, None] == jnp.arange(seq_count * capacity)[None, :]).astype(jnp.bfloat16)
    outgoing_back = jnp.einsum(
        "js,jkxf->skxf", placer, rand_terms, preferred_element_type=jnp.float32
    ).astype(jnp.bfloat16)
    arrived = lax.all_to_all(outgoing_back, "seq", split_axis=0, concat_axis=0, tiled=True)

    dscores_local = (probs_local * (grads_local - row_dot)).astype(jnp.bfloat16)
    low_local = probs_local.astype(jnp.bfloat16)
    query_grads = (
        jnp.einsum(
            "bhxky,bkyhd->bxhd", dscores_local, local_keys, preferred_element_type=jnp.float32
        )
        + jnp.einsum(
            "bhxky,bkyhd->bxhd", dscores_rand, rand_keys, preferred_element_type=jnp.float32
        )
    ) * score_scale
    key_terms = (
        jnp.einsum(
            "bhxky,bxhd->bkyhd", dscores_local, query_blocks, preferred_element_type=jnp.float32
        )
        * score_scale
    )
    value_terms = jnp.einsum(
        "bhxky,bxhd->bkyhd", low_local, dout_blocks, preferred_element_type=jnp.float32
    )
    pair_terms = jnp.stack([key_terms, value_terms]).reshape(
        2, per_dev, local_count, BLOCK, features
    )
    framed_sum = jnp.pad(pair_terms[:, :, 0], ((0, 0), (0, 2), (0, 0), (0, 0)))
    framed_sum = framed_sum + jnp.pad(pair_terms[:, :, 1], ((0, 0), (1, 1), (0, 0), (0, 0)))
    framed_sum = framed_sum + jnp.pad(pair_terms[:, :, 2], ((0, 0), (2, 0), (0, 0), (0, 0)))
    totals = framed_sum[:, 1 : per_dev + 1]
    global_sum = jnp.sum(pair_terms[:, :, 3 : 3 + G], axis=1)
    rim_terms = jnp.concatenate([framed_sum[:, 0], framed_sum[:, -1]], axis=1)
    widened = extended_2(rim_terms.astype(jnp.bfloat16), (("seq", 1),), BLOCK).astype(
        rim_terms.dtype
    )
    totals = totals.at[:, 0].add(widened[:, :BLOCK])
    totals = totals.at[:, per_dev - 1].add(widened[:, -BLOCK:])
    everywhere = reduce_to_first(global_sum, "seq")
    padded_global = jnp.pad(everywhere, ((0, 0), (0, per_dev - G), (0, 0), (0, 0))) * (
        device == 0
    ).astype(jnp.float32)
    totals = totals + padded_global
    collected = jnp.einsum(
        "dcb,dcsxf->sbxf",
        chooser.astype(jnp.bfloat16),
        arrived.reshape(seq_count, capacity, 2, BLOCK, features),
        preferred_element_type=jnp.float32,
    )
    totals = totals + collected
    return query_grads.reshape(tokens, features), totals


def on_device(query, key, value, grad_out, rand_blocks):
    stacked = jnp.stack([query, key, value, grad_out])
    stacked = lax.all_to_all(stacked, "head", split_axis=2, concat_axis=1, tiled=True)
    queries, keys, values, out_grads = stacked[0], stacked[1], stacked[2], stacked[3]
    tokens, features = queries.shape
    head_count = features // HD
    per_dev = tokens // BLOCK
    seq_count = lax.axis_size("seq")
    device = lax.axis_index("seq")
    capacity = (per_dev * R + seq_count - 3) // (seq_count - 2)
    rand_count = per_dev * R
    score_scale = HD ** (-0.5)
    requested = rand_blocks.reshape(seq_count, rand_count)
    owners_all, within_all, rank_all, usable_all = jax.vmap(
        lambda sender: request_plan(requested, sender, per_dev)
    )(jnp.arange(seq_count, dtype=jnp.int32))
    to_me = usable_all & (owners_all == device)
    slot_ids = jnp.arange(capacity)
    block_ids = jnp.arange(per_dev)
    matches = (
        to_me[:, :, None, None]
        & (rank_all[:, :, None, None] == slot_ids[None, None, :, None])
        & (within_all[:, :, None, None] == block_ids[None, None, None, :])
    )
    chooser = jnp.sum(matches.astype(jnp.float32), axis=1)
    my_owners, my_within, my_rank, my_usable = request_plan(requested, device, per_dev)
    my_slot = jnp.clip(my_owners, 0, seq_count - 1) * capacity + my_rank
    own_pairs = jnp.stack([keys, values]).reshape(2, per_dev, BLOCK, features)
    served = jnp.einsum(
        "dcb,sbxf->dcsxf",
        chooser.astype(jnp.bfloat16),
        own_pairs,
        preferred_element_type=jnp.float32,
    ).astype(jnp.bfloat16)
    outgoing = served.reshape(seq_count * capacity, 2, BLOCK, features)
    leading = jnp.stack([keys[: G * BLOCK], values[: G * BLOCK]])
    global_pairs = broadcast(leading, "seq", 0).reshape(2, G, BLOCK, features)
    extended = extended_2(jnp.stack([keys, values]), (("seq", 1),), BLOCK)
    outgoing, global_pairs, extended = lax.optimization_barrier((outgoing, global_pairs, extended))
    chunk_heads = 2 if head_count % 2 == 0 else 1
    chunk_width = chunk_heads * HD
    pieces = []
    for c0 in range(0, features, chunk_width):
        pieces.append(
            attend_chunk(
                queries[:, c0 : c0 + chunk_width],
                out_grads[:, c0 : c0 + chunk_width],
                own_pairs[..., c0 : c0 + chunk_width],
                outgoing[..., c0 : c0 + chunk_width],
                global_pairs[..., c0 : c0 + chunk_width],
                extended[..., c0 : c0 + chunk_width],
                chooser, my_slot, my_usable, device, seq_count, capacity,
            )
        )
    query_grads = jnp.concatenate([p[0] for p in pieces], axis=-1)
    totals = jnp.concatenate([p[1] for p in pieces], axis=-1)
    grad_rows = query_grads.reshape(tokens, features).astype(jnp.bfloat16)
    key_rows = totals[0].reshape(tokens, features).astype(jnp.bfloat16)
    value_rows = totals[1].reshape(tokens, features).astype(jnp.bfloat16)
    result = jnp.stack([grad_rows, key_rows, value_rows])
    result = lax.all_to_all(result, "head", split_axis=1, concat_axis=2, tiled=True)
    return (result[0], result[1], result[2])


def solution(mesh):
    in_specs = (
        P(("seq", "head"), None),
        P(("seq", "head"), None),
        P(("seq", "head"), None),
        P(("seq", "head"), None),
        P(),
    )
    out_specs = (P(("seq", "head"), None), P(("seq", "head"), None), P(("seq", "head"), None))
    return jax.shard_map(
        on_device, mesh=mesh, in_specs=in_specs, out_specs=out_specs, check_vma=False
    )
```

```python
import jax
import jax.numpy as jnp
from jax import lax
from jax.sharding import PartitionSpec as P

HD = 128
BLOCK = 64
G = 2
R = 3


big_negative = -1e30


def broadcast(block, axis, source):
    peers = lax.axis_size(axis)
    block = jnp.where(lax.axis_index(axis) == source, block, jnp.zeros_like(block))
    inner = 8 if peers % 8 == 0 else 1
    if inner > 1 and source == 0:
        outer = peers // inner
        received = [
            lax.ppermute(block, axis, [(0, k * inner)]) for k in range(1, outer)
        ]
        for part in received:
            block = block + part
        received = [
            lax.ppermute(block, axis, [(z * inner, z * inner + k) for z in range(outer)])
            for k in range(1, inner)
        ]
        for part in received:
            block = block + part
        return block
    step = 1
    while step * 2 < peers:
        step *= 2
    while step >= 1:
        pairs = [(i, i + step) for i in range(0, peers, 2 * step) if i + step < peers]
        block = block + lax.ppermute(block, axis, pairs)
        step //= 2
    return block


def reduce_to_first(block, axis):
    peers = lax.axis_size(axis)
    step = 1
    while step < peers:
        pairs = [(i + step, i) for i in range(0, peers, 2 * step) if i + step < peers]
        block = block + lax.ppermute(block, axis, pairs)
        step *= 2
    return block


def extended_2(shard, sides, width):
    for axis, dim in sides:
        peers, length = (lax.axis_size(axis), shard.shape[dim])
        up = [(i, (i + 1) % peers) for i in range(peers - 1)]
        down = [(j, i) for i, j in up]
        last = lax.slice_in_dim(shard, length - width, length, axis=dim)
        leading = lax.slice_in_dim(shard, 0, width, axis=dim)
        before = lax.ppermute(last, axis, up)
        after = lax.ppermute(leading, axis, down)
        shard = jnp.concatenate([before, shard, after], axis=dim)
    return shard


def request_plan(requested, device, per_dev):
    wanted_row = requested[device]
    owners = wanted_row // per_dev
    within = wanted_row % per_dev
    usable = jnp.ones(wanted_row.shape, jnp.bool_)
    positions = jnp.arange(owners.shape[0])
    earlier = (owners[:, None] == owners[None, :]) & (positions[None, :] < positions[:, None])
    slot_rank = jnp.sum(earlier.astype(jnp.int32), axis=1)
    return (owners, within, slot_rank, usable)


def attend_chunk(queries, out_grads, own_pairs, outgoing, global_pairs, extended,
                 chooser, my_slot, my_usable, device, seq_count, capacity, after=None):
    tokens, features = queries.shape
    head_count = features // HD
    per_dev = tokens // BLOCK
    rand_count = per_dev * R
    score_scale = HD ** (-0.5)
    incoming = lax.all_to_all(outgoing, "seq", split_axis=0, concat_axis=0, tiled=True)

    left_pair = extended[:, :BLOCK]
    right_pair = extended[:, -BLOCK:]
    framed = jnp.concatenate([left_pair[:, None], own_pairs, right_pair[:, None]], axis=1)
    window = jnp.stack(
        [framed[:, 0:per_dev], framed[:, 1 : per_dev + 1], framed[:, 2 : per_dev + 2]], axis=2
    )
    global_slots = jnp.broadcast_to(global_pairs[:, None], (2, per_dev, G, BLOCK, features))
    local = jnp.concatenate([window, global_slots], axis=2)
    local_count = 3 + G
    local_keys = local[0].reshape(per_dev, local_count, BLOCK, head_count, HD)
    local_values = local[1].reshape(per_dev, local_count, BLOCK, head_count, HD)
    block_index = device * per_dev + jnp.arange(per_dev)
    glob_index = jnp.arange(G)
    intersections = jnp.abs(glob_index[None, :] - block_index[:, None]) <= 1
    live_local = jnp.concatenate(
        [
            (block_index >= 1)[:, None],
            jnp.ones((per_dev, 1), jnp.bool_),
            (block_index <= seq_count * per_dev - 2)[:, None],
            jnp.logical_not(intersections),
        ],
        axis=1,
    )
    query_blocks = queries.reshape(per_dev, BLOCK, head_count, HD)
    dout_blocks = out_grads.reshape(per_dev, BLOCK, head_count, HD)
    scores_local = (
        jnp.einsum("bxhd,bkyhd->bhxky", query_blocks, local_keys, preferred_element_type=jnp.float32)
        * score_scale
    )
    scores_local = jnp.where(live_local[:, None, None, :, None], scores_local, big_negative)
    grads_local = jnp.einsum(
        "bxhd,bkyhd->bhxky", dout_blocks, local_values, preferred_element_type=jnp.float32
    )
    max_local = jnp.max(scores_local, axis=(3, 4), keepdims=True)

    fetched = incoming[my_slot]
    randoms = fetched.reshape(per_dev, R, 2, BLOCK, features)
    rand_keys = randoms[:, :, 0].reshape(per_dev, R, BLOCK, head_count, HD)
    rand_values = randoms[:, :, 1].reshape(per_dev, R, BLOCK, head_count, HD)
    scores_rand = (
        jnp.einsum("bxhd,bkyhd->bhxky", query_blocks, rand_keys, preferred_element_type=jnp.float32)
        * score_scale
    )
    grads_rand = jnp.einsum(
        "bxhd,bkyhd->bhxky", dout_blocks, rand_values, preferred_element_type=jnp.float32
    )
    row_max = jnp.maximum(max_local, jnp.max(scores_rand, axis=(3, 4), keepdims=True))
    weights_local = jnp.exp(scores_local - row_max)
    weights_rand = jnp.exp(scores_rand - row_max)
    row_total = jnp.sum(weights_local, axis=(3, 4), keepdims=True) + jnp.sum(
        weights_rand, axis=(3, 4), keepdims=True
    )
    probs_local = weights_local / row_total
    probs_rand = weights_rand / row_total
    row_dot = jnp.sum(probs_local * grads_local, axis=(3, 4), keepdims=True) + jnp.sum(
        probs_rand * grads_rand, axis=(3, 4), keepdims=True
    )
    dscores_rand = (probs_rand * (grads_rand - row_dot)).astype(jnp.bfloat16)
    low_rand = probs_rand.astype(jnp.bfloat16)
    key_rand = (
        jnp.einsum(
            "bhxky,bxhd->bkyhd", dscores_rand, query_blocks, preferred_element_type=jnp.float32
        )
        * score_scale
    )
    value_rand = jnp.einsum(
        "bhxky,bxhd->bkyhd", low_rand, dout_blocks, preferred_element_type=jnp.float32
    )
    rand_terms = (
        jnp.stack([key_rand, value_rand])
        .reshape(2, rand_count, BLOCK, features)
        .transpose(1, 0, 2, 3)
        .astype(jnp.bfloat16)
    )
    target = jnp.where(my_usable, my_slot, seq_count * capacity)
    placer = (target[:, None] == jnp.arange(seq_count * capacity)[None, :]).astype(jnp.bfloat16)
    outgoing_back = jnp.einsum(
        "js,jkxf->skxf", placer, rand_terms, preferred_element_type=jnp.float32
    ).astype(jnp.bfloat16)
    if after is not None:
        outgoing_back, after = lax.optimization_barrier((outgoing_back, after))
    arrived = lax.all_to_all(outgoing_back, "seq", split_axis=0, concat_axis=0, tiled=True)

    dscores_local = (probs_local * (grads_local - row_dot)).astype(jnp.bfloat16)
    low_local = probs_local.astype(jnp.bfloat16)
    query_grads = (
        jnp.einsum(
            "bhxky,bkyhd->bxhd", dscores_local, local_keys, preferred_element_type=jnp.float32
        )
        + jnp.einsum(
            "bhxky,bkyhd->bxhd", dscores_rand, rand_keys, preferred_element_type=jnp.float32
        )
    ) * score_scale
    key_global = (
        jnp.einsum(
            "bhxky,bxhd->kyhd",
            dscores_local[:, :, :, 3:],
            query_blocks,
            preferred_element_type=jnp.float32,
        )
        * score_scale
    )
    value_global = jnp.einsum(
        "bhxky,bxhd->kyhd", low_local[:, :, :, 3:], dout_blocks, preferred_element_type=jnp.float32
    )
    global_sum = jnp.stack([key_global, value_global]).reshape(2, G, BLOCK, features)
    everywhere = reduce_to_first(global_sum, "seq")
    key_terms = (
        jnp.einsum(
            "bhxky,bxhd->bkyhd",
            dscores_local[:, :, :, :3],
            query_blocks,
            preferred_element_type=jnp.float32,
        )
        * score_scale
    )
    value_terms = jnp.einsum(
        "bhxky,bxhd->bkyhd", low_local[:, :, :, :3], dout_blocks, preferred_element_type=jnp.float32
    )
    pair_terms = jnp.stack([key_terms, value_terms]).reshape(2, per_dev, 3, BLOCK, features)
    framed_sum = jnp.pad(pair_terms[:, :, 0], ((0, 0), (0, 2), (0, 0), (0, 0)))
    framed_sum = framed_sum + jnp.pad(pair_terms[:, :, 1], ((0, 0), (1, 1), (0, 0), (0, 0)))
    framed_sum = framed_sum + jnp.pad(pair_terms[:, :, 2], ((0, 0), (2, 0), (0, 0), (0, 0)))
    totals = framed_sum[:, 1 : per_dev + 1]
    rim_terms = jnp.concatenate([framed_sum[:, 0], framed_sum[:, -1]], axis=1)
    widened = extended_2(rim_terms.astype(jnp.bfloat16), (("seq", 1),), BLOCK).astype(
        rim_terms.dtype
    )
    totals = totals.at[:, 0].add(widened[:, :BLOCK])
    totals = totals.at[:, per_dev - 1].add(widened[:, -BLOCK:])
    padded_global = jnp.pad(everywhere, ((0, 0), (0, per_dev - G), (0, 0), (0, 0))) * (
        device == 0
    ).astype(jnp.float32)
    totals = totals + padded_global
    collected = jnp.einsum(
        "dcb,dcsxf->sbxf",
        chooser.astype(jnp.bfloat16),
        arrived.reshape(seq_count, capacity, 2, BLOCK, features),
        preferred_element_type=jnp.float32,
    )
    totals = totals + collected
    return query_grads.reshape(tokens, features), totals, everywhere


def on_device(query, key, value, grad_out, rand_blocks):
    stacked = jnp.stack([query, key, value, grad_out])
    stacked = lax.all_to_all(stacked, "head", split_axis=2, concat_axis=1, tiled=True)
    queries, keys, values, out_grads = stacked[0], stacked[1], stacked[2], stacked[3]
    tokens, features = queries.shape
    head_count = features // HD
    per_dev = tokens // BLOCK
    seq_count = lax.axis_size("seq")
    device = lax.axis_index("seq")
    capacity = (per_dev * R + seq_count - 3) // (seq_count - 2)
    rand_count = per_dev * R
    score_scale = HD ** (-0.5)
    requested = rand_blocks.reshape(seq_count, rand_count)
    owners_all, within_all, rank_all, usable_all = jax.vmap(
        lambda sender: request_plan(requested, sender, per_dev)
    )(jnp.arange(seq_count, dtype=jnp.int32))
    to_me = usable_all & (owners_all == device)
    slot_ids = jnp.arange(capacity)
    block_ids = jnp.arange(per_dev)
    matches = (
        to_me[:, :, None, None]
        & (rank_all[:, :, None, None] == slot_ids[None, None, :, None])
        & (within_all[:, :, None, None] == block_ids[None, None, None, :])
    )
    chooser = jnp.sum(matches.astype(jnp.float32), axis=1)
    my_owners, my_within, my_rank, my_usable = request_plan(requested, device, per_dev)
    my_slot = jnp.clip(my_owners, 0, seq_count - 1) * capacity + my_rank
    own_pairs = jnp.stack([keys, values]).reshape(2, per_dev, BLOCK, features)
    served = jnp.einsum(
        "dcb,sbxf->dcsxf",
        chooser.astype(jnp.bfloat16),
        own_pairs,
        preferred_element_type=jnp.float32,
    ).astype(jnp.bfloat16)
    outgoing = served.reshape(seq_count * capacity, 2, BLOCK, features)
    leading = jnp.stack([keys[: G * BLOCK], values[: G * BLOCK]])
    global_pairs = broadcast(leading, "seq", 0).reshape(2, G, BLOCK, features)
    extended = extended_2(jnp.stack([keys, values]), (("seq", 1),), BLOCK)
    outgoing, global_pairs, extended = lax.optimization_barrier((outgoing, global_pairs, extended))
    chunk_heads = 2 if head_count % 2 == 0 else 1
    chunk_width = chunk_heads * HD
    pieces = []
    for c0 in range(0, features, chunk_width):
        pieces.append(
            attend_chunk(
                queries[:, c0 : c0 + chunk_width],
                out_grads[:, c0 : c0 + chunk_width],
                own_pairs[..., c0 : c0 + chunk_width],
                outgoing[..., c0 : c0 + chunk_width],
                global_pairs[..., c0 : c0 + chunk_width],
                extended[..., c0 : c0 + chunk_width],
                chooser, my_slot, my_usable, device, seq_count, capacity,
                after=pieces[-1][2] if pieces else None,
            )
        )
    query_grads = jnp.concatenate([p[0] for p in pieces], axis=-1)
    totals = jnp.concatenate([p[1] for p in pieces], axis=-1)
    grad_rows = query_grads.reshape(tokens, features).astype(jnp.bfloat16)
    key_rows = totals[0].reshape(tokens, features).astype(jnp.bfloat16)
    value_rows = totals[1].reshape(tokens, features).astype(jnp.bfloat16)
    result = jnp.stack([grad_rows, key_rows, value_rows])
    result = lax.all_to_all(result, "head", split_axis=1, concat_axis=2, tiled=True)
    return (result[0], result[1], result[2])


def solution(mesh):
    in_specs = (
        P(("seq", "head"), None),
        P(("seq", "head"), None),
        P(("seq", "head"), None),
        P(("seq", "head"), None),
        P(),
    )
    out_specs = (P(("seq", "head"), None), P(("seq", "head"), None), P(("seq", "head"), None))
    return jax.shard_map(
        on_device, mesh=mesh, in_specs=in_specs, out_specs=out_specs, check_vma=False
    )
```

```python
import jax
import jax.numpy as jnp
from jax import lax
from jax.sharding import PartitionSpec as P

HD = 128
BLOCK = 64
G = 2
R = 3


big_negative = -1e30


def broadcast(block, axis, source):
    peers = lax.axis_size(axis)
    block = jnp.where(lax.axis_index(axis) == source, block, jnp.zeros_like(block))
    inner = 8 if peers % 8 == 0 else 1
    if inner > 1 and source == 0:
        outer = peers // inner
        received = [
            lax.ppermute(block, axis, [(0, k * inner)]) for k in range(1, outer)
        ]
        for part in received:
            block = block + part
        received = [
            lax.ppermute(block, axis, [(z * inner, z * inner + k) for z in range(outer)])
            for k in range(1, inner)
        ]
        for part in received:
            block = block + part
        return block
    step = 1
    while step * 2 < peers:
        step *= 2
    while step >= 1:
        pairs = [(i, i + step) for i in range(0, peers, 2 * step) if i + step < peers]
        block = block + lax.ppermute(block, axis, pairs)
        step //= 2
    return block


def reduce_to_first(block, axis):
    peers = lax.axis_size(axis)
    step = 1
    while step < peers:
        radix = 4 if peers % (step * 4) == 0 else 2
        received = [
            lax.ppermute(
                block, axis, [(i + k * step, i) for i in range(0, peers, radix * step)]
            )
            for k in range(1, radix)
        ]
        for part in received:
            block = block + part
        step *= radix
    return block


def extended_2(shard, sides, width):
    for axis, dim in sides:
        peers, length = (lax.axis_size(axis), shard.shape[dim])
        up = [(i, (i + 1) % peers) for i in range(peers - 1)]
        down = [(j, i) for i, j in up]
        last = lax.slice_in_dim(shard, length - width, length, axis=dim)
        leading = lax.slice_in_dim(shard, 0, width, axis=dim)
        before = lax.ppermute(last, axis, up)
        after = lax.ppermute(leading, axis, down)
        shard = jnp.concatenate([before, shard, after], axis=dim)
    return shard


def request_plan(requested, device, per_dev):
    wanted_row = requested[device]
    owners = wanted_row // per_dev
    within = wanted_row % per_dev
    usable = jnp.ones(wanted_row.shape, jnp.bool_)
    positions = jnp.arange(owners.shape[0])
    earlier = (owners[:, None] == owners[None, :]) & (positions[None, :] < positions[:, None])
    slot_rank = jnp.sum(earlier.astype(jnp.int32), axis=1)
    return (owners, within, slot_rank, usable)


def attend_chunk(queries, out_grads, own_pairs, outgoing, global_pairs, extended,
                 chooser, my_slot, my_usable, device, seq_count, capacity, after=None):
    tokens, features = queries.shape
    head_count = features // HD
    per_dev = tokens // BLOCK
    rand_count = per_dev * R
    score_scale = HD ** (-0.5)
    incoming = lax.all_to_all(outgoing, "seq", split_axis=0, concat_axis=0, tiled=True)

    left_pair = extended[:, :BLOCK]
    right_pair = extended[:, -BLOCK:]
    framed = jnp.concatenate([left_pair[:, None], own_pairs, right_pair[:, None]], axis=1)
    window = jnp.stack(
        [framed[:, 0:per_dev], framed[:, 1 : per_dev + 1], framed[:, 2 : per_dev + 2]], axis=2
    )
    global_slots = jnp.broadcast_to(global_pairs[:, None], (2, per_dev, G, BLOCK, features))
    local = jnp.concatenate([window, global_slots], axis=2)
    local_count = 3 + G
    local_keys = local[0].reshape(per_dev, local_count, BLOCK, head_count, HD)
    local_values = local[1].reshape(per_dev, local_count, BLOCK, head_count, HD)
    block_index = device * per_dev + jnp.arange(per_dev)
    glob_index = jnp.arange(G)
    intersections = jnp.abs(glob_index[None, :] - block_index[:, None]) <= 1
    live_local = jnp.concatenate(
        [
            (block_index >= 1)[:, None],
            jnp.ones((per_dev, 1), jnp.bool_),
            (block_index <= seq_count * per_dev - 2)[:, None],
            jnp.logical_not(intersections),
        ],
        axis=1,
    )
    query_blocks = queries.reshape(per_dev, BLOCK, head_count, HD)
    dout_blocks = out_grads.reshape(per_dev, BLOCK, head_count, HD)
    scores_local = (
        jnp.einsum("bxhd,bkyhd->bhxky", query_blocks, local_keys, preferred_element_type=jnp.float32)
        * score_scale
    )
    scores_local = jnp.where(live_local[:, None, None, :, None], scores_local, big_negative)
    grads_local = jnp.einsum(
        "bxhd,bkyhd->bhxky", dout_blocks, local_values, preferred_element_type=jnp.float32
    )
    max_local = jnp.max(scores_local, axis=(3, 4), keepdims=True)

    fetched = incoming[my_slot]
    randoms = fetched.reshape(per_dev, R, 2, BLOCK, features)
    rand_keys = randoms[:, :, 0].reshape(per_dev, R, BLOCK, head_count, HD)
    rand_values = randoms[:, :, 1].reshape(per_dev, R, BLOCK, head_count, HD)
    scores_rand = (
        jnp.einsum("bxhd,bkyhd->bhxky", query_blocks, rand_keys, preferred_element_type=jnp.float32)
        * score_scale
    )
    grads_rand = jnp.einsum(
        "bxhd,bkyhd->bhxky", dout_blocks, rand_values, preferred_element_type=jnp.float32
    )
    row_max = jnp.maximum(max_local, jnp.max(scores_rand, axis=(3, 4), keepdims=True))
    weights_local = jnp.exp(scores_local - row_max)
    weights_rand = jnp.exp(scores_rand - row_max)
    row_total = jnp.sum(weights_local, axis=(3, 4), keepdims=True) + jnp.sum(
        weights_rand, axis=(3, 4), keepdims=True
    )
    probs_local = weights_local / row_total
    probs_rand = weights_rand / row_total
    row_dot = jnp.sum(probs_local * grads_local, axis=(3, 4), keepdims=True) + jnp.sum(
        probs_rand * grads_rand, axis=(3, 4), keepdims=True
    )
    dscores_rand = (probs_rand * (grads_rand - row_dot)).astype(jnp.bfloat16)
    low_rand = probs_rand.astype(jnp.bfloat16)
    key_rand = (
        jnp.einsum(
            "bhxky,bxhd->bkyhd", dscores_rand, query_blocks, preferred_element_type=jnp.float32
        )
        * score_scale
    )
    value_rand = jnp.einsum(
        "bhxky,bxhd->bkyhd", low_rand, dout_blocks, preferred_element_type=jnp.float32
    )
    rand_terms = (
        jnp.stack([key_rand, value_rand])
        .reshape(2, rand_count, BLOCK, features)
        .transpose(1, 0, 2, 3)
        .astype(jnp.bfloat16)
    )
    target = jnp.where(my_usable, my_slot, seq_count * capacity)
    placer = (target[:, None] == jnp.arange(seq_count * capacity)[None, :]).astype(jnp.bfloat16)
    outgoing_back = jnp.einsum(
        "js,jkxf->skxf", placer, rand_terms, preferred_element_type=jnp.float32
    ).astype(jnp.bfloat16)
    if after is not None:
        outgoing_back, after = lax.optimization_barrier((outgoing_back, after))
    arrived = lax.all_to_all(outgoing_back, "seq", split_axis=0, concat_axis=0, tiled=True)

    dscores_local = (probs_local * (grads_local - row_dot)).astype(jnp.bfloat16)
    low_local = probs_local.astype(jnp.bfloat16)
    query_grads = (
        jnp.einsum(
            "bhxky,bkyhd->bxhd", dscores_local, local_keys, preferred_element_type=jnp.float32
        )
        + jnp.einsum(
            "bhxky,bkyhd->bxhd", dscores_rand, rand_keys, preferred_element_type=jnp.float32
        )
    ) * score_scale
    key_global = (
        jnp.einsum(
            "bhxky,bxhd->kyhd",
            dscores_local[:, :, :, 3:],
            query_blocks,
            preferred_element_type=jnp.float32,
        )
        * score_scale
    )
    value_global = jnp.einsum(
        "bhxky,bxhd->kyhd", low_local[:, :, :, 3:], dout_blocks, preferred_element_type=jnp.float32
    )
    global_sum = jnp.stack([key_global, value_global]).reshape(2, G, BLOCK, features)
    everywhere = reduce_to_first(global_sum, "seq")
    key_terms = (
        jnp.einsum(
            "bhxky,bxhd->bkyhd",
            dscores_local[:, :, :, :3],
            query_blocks,
            preferred_element_type=jnp.float32,
        )
        * score_scale
    )
    value_terms = jnp.einsum(
        "bhxky,bxhd->bkyhd", low_local[:, :, :, :3], dout_blocks, preferred_element_type=jnp.float32
    )
    pair_terms = jnp.stack([key_terms, value_terms]).reshape(2, per_dev, 3, BLOCK, features)
    framed_sum = jnp.pad(pair_terms[:, :, 0], ((0, 0), (0, 2), (0, 0), (0, 0)))
    framed_sum = framed_sum + jnp.pad(pair_terms[:, :, 1], ((0, 0), (1, 1), (0, 0), (0, 0)))
    framed_sum = framed_sum + jnp.pad(pair_terms[:, :, 2], ((0, 0), (2, 0), (0, 0), (0, 0)))
    totals = framed_sum[:, 1 : per_dev + 1]
    rim_terms = jnp.concatenate([framed_sum[:, 0], framed_sum[:, -1]], axis=1)
    widened = extended_2(rim_terms.astype(jnp.bfloat16), (("seq", 1),), BLOCK).astype(
        rim_terms.dtype
    )
    totals = totals.at[:, 0].add(widened[:, :BLOCK])
    totals = totals.at[:, per_dev - 1].add(widened[:, -BLOCK:])
    padded_global = jnp.pad(everywhere, ((0, 0), (0, per_dev - G), (0, 0), (0, 0))) * (
        device == 0
    ).astype(jnp.float32)
    totals = totals + padded_global
    collected = jnp.einsum(
        "dcb,dcsxf->sbxf",
        chooser.astype(jnp.bfloat16),
        arrived.reshape(seq_count, capacity, 2, BLOCK, features),
        preferred_element_type=jnp.float32,
    )
    totals = totals + collected
    return query_grads.reshape(tokens, features), totals, everywhere


def on_device(query, key, value, grad_out, rand_blocks):
    kv_stacked = jnp.stack([key, value])
    kv_stacked = lax.all_to_all(kv_stacked, "head", split_axis=2, concat_axis=1, tiled=True)
    keys, values = kv_stacked[0], kv_stacked[1]
    qo_stacked = jnp.stack([query, grad_out])
    qo_stacked = lax.all_to_all(qo_stacked, "head", split_axis=2, concat_axis=1, tiled=True)
    queries, out_grads = qo_stacked[0], qo_stacked[1]
    tokens, features = queries.shape
    head_count = features // HD
    per_dev = tokens // BLOCK
    seq_count = lax.axis_size("seq")
    device = lax.axis_index("seq")
    capacity = (per_dev * R + seq_count - 3) // (seq_count - 2)
    rand_count = per_dev * R
    score_scale = HD ** (-0.5)
    requested = rand_blocks.reshape(seq_count, rand_count)
    owners_all, within_all, rank_all, usable_all = jax.vmap(
        lambda sender: request_plan(requested, sender, per_dev)
    )(jnp.arange(seq_count, dtype=jnp.int32))
    to_me = usable_all & (owners_all == device)
    slot_ids = jnp.arange(capacity)
    block_ids = jnp.arange(per_dev)
    matches = (
        to_me[:, :, None, None]
        & (rank_all[:, :, None, None] == slot_ids[None, None, :, None])
        & (within_all[:, :, None, None] == block_ids[None, None, None, :])
    )
    chooser = jnp.sum(matches.astype(jnp.float32), axis=1)
    my_owners, my_within, my_rank, my_usable = request_plan(requested, device, per_dev)
    my_slot = jnp.clip(my_owners, 0, seq_count - 1) * capacity + my_rank
    own_pairs = jnp.stack([keys, values]).reshape(2, per_dev, BLOCK, features)
    served = jnp.einsum(
        "dcb,sbxf->dcsxf",
        chooser.astype(jnp.bfloat16),
        own_pairs,
        preferred_element_type=jnp.float32,
    ).astype(jnp.bfloat16)
    outgoing = served.reshape(seq_count * capacity, 2, BLOCK, features)
    leading = jnp.stack([keys[: G * BLOCK], values[: G * BLOCK]])
    global_pairs = broadcast(leading, "seq", 0).reshape(2, G, BLOCK, features)
    extended = extended_2(jnp.stack([keys, values]), (("seq", 1),), BLOCK)
    outgoing, global_pairs, extended = lax.optimization_barrier((outgoing, global_pairs, extended))
    chunk_heads = 2 if head_count % 2 == 0 else 1
    chunk_width = chunk_heads * HD
    pieces = []
    for c0 in range(0, features, chunk_width):
        pieces.append(
            attend_chunk(
                queries[:, c0 : c0 + chunk_width],
                out_grads[:, c0 : c0 + chunk_width],
                own_pairs[..., c0 : c0 + chunk_width],
                outgoing[..., c0 : c0 + chunk_width],
                global_pairs[..., c0 : c0 + chunk_width],
                extended[..., c0 : c0 + chunk_width],
                chooser, my_slot, my_usable, device, seq_count, capacity,
            )
        )
    query_grads = jnp.concatenate([p[0] for p in pieces], axis=-1)
    totals = jnp.concatenate([p[1] for p in pieces], axis=-1)
    grad_rows = query_grads.reshape(tokens, features).astype(jnp.bfloat16)
    key_rows = totals[0].reshape(tokens, features).astype(jnp.bfloat16)
    value_rows = totals[1].reshape(tokens, features).astype(jnp.bfloat16)
    result = jnp.stack([grad_rows, key_rows, value_rows])
    result = lax.all_to_all(result, "head", split_axis=1, concat_axis=2, tiled=True)
    return (result[0], result[1], result[2])


def solution(mesh):
    in_specs = (
        P(("seq", "head"), None),
        P(("seq", "head"), None),
        P(("seq", "head"), None),
        P(("seq", "head"), None),
        P(),
    )
    out_specs = (P(("seq", "head"), None), P(("seq", "head"), None), P(("seq", "head"), None))
    return jax.shard_map(
        on_device, mesh=mesh, in_specs=in_specs, out_specs=out_specs, check_vma=False
    )
```

```python
import jax
import jax.numpy as jnp
from jax import lax
from jax.sharding import PartitionSpec as P

HD = 128
BLOCK = 64
G = 2
R = 3


big_negative = -1e30


def broadcast(block, axis, source):
    peers = lax.axis_size(axis)
    block = jnp.where(lax.axis_index(axis) == source, block, jnp.zeros_like(block))
    inner = 8 if peers % 8 == 0 else 1
    if inner > 1 and source == 0:
        outer = peers // inner
        received = [
            lax.ppermute(block, axis, [(0, k * inner)]) for k in range(1, outer)
        ]
        for part in received:
            block = block + part
        received = [
            lax.ppermute(block, axis, [(z * inner, z * inner + k) for z in range(outer)])
            for k in range(1, inner)
        ]
        for part in received:
            block = block + part
        return block
    step = 1
    while step * 2 < peers:
        step *= 2
    while step >= 1:
        pairs = [(i, i + step) for i in range(0, peers, 2 * step) if i + step < peers]
        block = block + lax.ppermute(block, axis, pairs)
        step //= 2
    return block


def reduce_to_first(block, axis):
    peers = lax.axis_size(axis)
    step = 1
    while step < peers:
        radix = 4 if peers % (step * 4) == 0 else 2
        received = [
            lax.ppermute(
                block, axis, [(i + k * step, i) for i in range(0, peers, radix * step)]
            )
            for k in range(1, radix)
        ]
        for part in received:
            block = block + part
        step *= radix
    return block


def gather_sum_to_first(block, axis):
    peers = lax.axis_size(axis)
    flat = block.reshape(-1)
    width = -(-flat.shape[0] // peers)
    flat = jnp.pad(flat, (0, width * peers - flat.shape[0])).reshape(peers, width)
    parts = lax.all_to_all(flat, axis, split_axis=0, concat_axis=0, tiled=True)
    mine = jnp.sum(parts, axis=0)
    outgoing = jnp.pad(mine[None], ((0, peers - 1), (0, 0)))
    gathered = lax.all_to_all(outgoing, axis, split_axis=0, concat_axis=0, tiled=True)
    return gathered.reshape(-1)[: block.size].reshape(block.shape)


def extended_2(shard, sides, width):
    for axis, dim in sides:
        peers, length = (lax.axis_size(axis), shard.shape[dim])
        up = [(i, (i + 1) % peers) for i in range(peers - 1)]
        down = [(j, i) for i, j in up]
        last = lax.slice_in_dim(shard, length - width, length, axis=dim)
        leading = lax.slice_in_dim(shard, 0, width, axis=dim)
        before = lax.ppermute(last, axis, up)
        after = lax.ppermute(leading, axis, down)
        shard = jnp.concatenate([before, shard, after], axis=dim)
    return shard


def request_plan(requested, device, per_dev):
    wanted_row = requested[device]
    owners = wanted_row // per_dev
    within = wanted_row % per_dev
    usable = jnp.ones(wanted_row.shape, jnp.bool_)
    positions = jnp.arange(owners.shape[0])
    earlier = (owners[:, None] == owners[None, :]) & (positions[None, :] < positions[:, None])
    slot_rank = jnp.sum(earlier.astype(jnp.int32), axis=1)
    return (owners, within, slot_rank, usable)


def attend_chunk(queries, out_grads, own_pairs, outgoing, global_pairs, extended,
                 chooser, my_slot, my_usable, device, seq_count, capacity, after=None):
    tokens, features = queries.shape
    head_count = features // HD
    per_dev = tokens // BLOCK
    rand_count = per_dev * R
    score_scale = HD ** (-0.5)
    incoming = lax.all_to_all(outgoing, "seq", split_axis=0, concat_axis=0, tiled=True)

    left_pair = extended[:, :BLOCK]
    right_pair = extended[:, -BLOCK:]
    framed = jnp.concatenate([left_pair[:, None], own_pairs, right_pair[:, None]], axis=1)
    window = jnp.stack(
        [framed[:, 0:per_dev], framed[:, 1 : per_dev + 1], framed[:, 2 : per_dev + 2]], axis=2
    )
    global_slots = jnp.broadcast_to(global_pairs[:, None], (2, per_dev, G, BLOCK, features))
    local = jnp.concatenate([window, global_slots], axis=2)
    local_count = 3 + G
    local_keys = local[0].reshape(per_dev, local_count, BLOCK, head_count, HD)
    local_values = local[1].reshape(per_dev, local_count, BLOCK, head_count, HD)
    block_index = device * per_dev + jnp.arange(per_dev)
    glob_index = jnp.arange(G)
    intersections = jnp.abs(glob_index[None, :] - block_index[:, None]) <= 1
    live_local = jnp.concatenate(
        [
            (block_index >= 1)[:, None],
            jnp.ones((per_dev, 1), jnp.bool_),
            (block_index <= seq_count * per_dev - 2)[:, None],
            jnp.logical_not(intersections),
        ],
        axis=1,
    )
    query_blocks = queries.reshape(per_dev, BLOCK, head_count, HD)
    dout_blocks = out_grads.reshape(per_dev, BLOCK, head_count, HD)
    scores_local = (
        jnp.einsum("bxhd,bkyhd->bhxky", query_blocks, local_keys, preferred_element_type=jnp.float32)
        * score_scale
    )
    scores_local = jnp.where(live_local[:, None, None, :, None], scores_local, big_negative)
    grads_local = jnp.einsum(
        "bxhd,bkyhd->bhxky", dout_blocks, local_values, preferred_element_type=jnp.float32
    )
    max_local = jnp.max(scores_local, axis=(3, 4), keepdims=True)

    fetched = incoming[my_slot]
    randoms = fetched.reshape(per_dev, R, 2, BLOCK, features)
    rand_keys = randoms[:, :, 0].reshape(per_dev, R, BLOCK, head_count, HD)
    rand_values = randoms[:, :, 1].reshape(per_dev, R, BLOCK, head_count, HD)
    scores_rand = (
        jnp.einsum("bxhd,bkyhd->bhxky", query_blocks, rand_keys, preferred_element_type=jnp.float32)
        * score_scale
    )
    grads_rand = jnp.einsum(
        "bxhd,bkyhd->bhxky", dout_blocks, rand_values, preferred_element_type=jnp.float32
    )
    row_max = jnp.maximum(max_local, jnp.max(scores_rand, axis=(3, 4), keepdims=True))
    weights_local = jnp.exp(scores_local - row_max)
    weights_rand = jnp.exp(scores_rand - row_max)
    row_total = jnp.sum(weights_local, axis=(3, 4), keepdims=True) + jnp.sum(
        weights_rand, axis=(3, 4), keepdims=True
    )
    probs_local = weights_local / row_total
    probs_rand = weights_rand / row_total
    row_dot = jnp.sum(probs_local * grads_local, axis=(3, 4), keepdims=True) + jnp.sum(
        probs_rand * grads_rand, axis=(3, 4), keepdims=True
    )
    dscores_rand = (probs_rand * (grads_rand - row_dot)).astype(jnp.bfloat16)
    low_rand = probs_rand.astype(jnp.bfloat16)
    key_rand = (
        jnp.einsum(
            "bhxky,bxhd->bkyhd", dscores_rand, query_blocks, preferred_element_type=jnp.float32
        )
        * score_scale
    )
    value_rand = jnp.einsum(
        "bhxky,bxhd->bkyhd", low_rand, dout_blocks, preferred_element_type=jnp.float32
    )
    rand_terms = (
        jnp.stack([key_rand, value_rand])
        .reshape(2, rand_count, BLOCK, features)
        .transpose(1, 0, 2, 3)
        .astype(jnp.bfloat16)
    )
    target = jnp.where(my_usable, my_slot, seq_count * capacity)
    placer = (target[:, None] == jnp.arange(seq_count * capacity)[None, :]).astype(jnp.bfloat16)
    outgoing_back = jnp.einsum(
        "js,jkxf->skxf", placer, rand_terms, preferred_element_type=jnp.float32
    ).astype(jnp.bfloat16)
    if after is not None:
        outgoing_back, after = lax.optimization_barrier((outgoing_back, after))
    arrived = lax.all_to_all(outgoing_back, "seq", split_axis=0, concat_axis=0, tiled=True)

    dscores_local = (probs_local * (grads_local - row_dot)).astype(jnp.bfloat16)
    low_local = probs_local.astype(jnp.bfloat16)
    query_grads = (
        jnp.einsum(
            "bhxky,bkyhd->bxhd", dscores_local, local_keys, preferred_element_type=jnp.float32
        )
        + jnp.einsum(
            "bhxky,bkyhd->bxhd", dscores_rand, rand_keys, preferred_element_type=jnp.float32
        )
    ) * score_scale
    key_global = (
        jnp.einsum(
            "bhxky,bxhd->kyhd",
            dscores_local[:, :, :, 3:],
            query_blocks,
            preferred_element_type=jnp.float32,
        )
        * score_scale
    )
    value_global = jnp.einsum(
        "bhxky,bxhd->kyhd", low_local[:, :, :, 3:], dout_blocks, preferred_element_type=jnp.float32
    )
    global_sum = jnp.stack([key_global, value_global]).reshape(2, G, BLOCK, features)
    key_terms = (
        jnp.einsum(
            "bhxky,bxhd->bkyhd",
            dscores_local[:, :, :, :3],
            query_blocks,
            preferred_element_type=jnp.float32,
        )
        * score_scale
    )
    value_terms = jnp.einsum(
        "bhxky,bxhd->bkyhd", low_local[:, :, :, :3], dout_blocks, preferred_element_type=jnp.float32
    )
    pair_terms = jnp.stack([key_terms, value_terms]).reshape(2, per_dev, 3, BLOCK, features)
    framed_sum = jnp.pad(pair_terms[:, :, 0], ((0, 0), (0, 2), (0, 0), (0, 0)))
    framed_sum = framed_sum + jnp.pad(pair_terms[:, :, 1], ((0, 0), (1, 1), (0, 0), (0, 0)))
    framed_sum = framed_sum + jnp.pad(pair_terms[:, :, 2], ((0, 0), (2, 0), (0, 0), (0, 0)))
    totals = framed_sum[:, 1 : per_dev + 1]
    rim_terms = jnp.concatenate([framed_sum[:, 0], framed_sum[:, -1]], axis=1)
    widened = extended_2(rim_terms.astype(jnp.bfloat16), (("seq", 1),), BLOCK).astype(
        rim_terms.dtype
    )
    totals = totals.at[:, 0].add(widened[:, :BLOCK])
    totals = totals.at[:, per_dev - 1].add(widened[:, -BLOCK:])
    collected = jnp.einsum(
        "dcb,dcsxf->sbxf",
        chooser.astype(jnp.bfloat16),
        arrived.reshape(seq_count, capacity, 2, BLOCK, features),
        preferred_element_type=jnp.float32,
    )
    totals = totals + collected
    return query_grads.reshape(tokens, features), totals, global_sum


def on_device(query, key, value, grad_out, rand_blocks):
    kv_stacked = jnp.stack([key, value])
    kv_stacked = lax.all_to_all(kv_stacked, "head", split_axis=2, concat_axis=1, tiled=True)
    keys, values = kv_stacked[0], kv_stacked[1]
    qo_stacked = jnp.stack([query, grad_out])
    qo_stacked = lax.all_to_all(qo_stacked, "head", split_axis=2, concat_axis=1, tiled=True)
    queries, out_grads = qo_stacked[0], qo_stacked[1]
    tokens, features = queries.shape
    head_count = features // HD
    per_dev = tokens // BLOCK
    seq_count = lax.axis_size("seq")
    device = lax.axis_index("seq")
    capacity = (per_dev * R + seq_count - 3) // (seq_count - 2)
    rand_count = per_dev * R
    score_scale = HD ** (-0.5)
    requested = rand_blocks.reshape(seq_count, rand_count)
    owners_all, within_all, rank_all, usable_all = jax.vmap(
        lambda sender: request_plan(requested, sender, per_dev)
    )(jnp.arange(seq_count, dtype=jnp.int32))
    to_me = usable_all & (owners_all == device)
    slot_ids = jnp.arange(capacity)
    block_ids = jnp.arange(per_dev)
    matches = (
        to_me[:, :, None, None]
        & (rank_all[:, :, None, None] == slot_ids[None, None, :, None])
        & (within_all[:, :, None, None] == block_ids[None, None, None, :])
    )
    chooser = jnp.sum(matches.astype(jnp.float32), axis=1)
    my_owners, my_within, my_rank, my_usable = request_plan(requested, device, per_dev)
    my_slot = jnp.clip(my_owners, 0, seq_count - 1) * capacity + my_rank
    own_pairs = jnp.stack([keys, values]).reshape(2, per_dev, BLOCK, features)
    served = jnp.einsum(
        "dcb,sbxf->dcsxf",
        chooser.astype(jnp.bfloat16),
        own_pairs,
        preferred_element_type=jnp.float32,
    ).astype(jnp.bfloat16)
    outgoing = served.reshape(seq_count * capacity, 2, BLOCK, features)
    leading = jnp.stack([keys[: G * BLOCK], values[: G * BLOCK]])
    global_pairs = broadcast(leading, "seq", 0).reshape(2, G, BLOCK, features)
    extended = extended_2(jnp.stack([keys, values]), (("seq", 1),), BLOCK)
    outgoing, global_pairs, extended = lax.optimization_barrier((outgoing, global_pairs, extended))
    chunk_heads = 2 if head_count % 2 == 0 else 1
    chunk_width = chunk_heads * HD
    pieces = []
    for c0 in range(0, features, chunk_width):
        pieces.append(
            attend_chunk(
                queries[:, c0 : c0 + chunk_width],
                out_grads[:, c0 : c0 + chunk_width],
                own_pairs[..., c0 : c0 + chunk_width],
                outgoing[..., c0 : c0 + chunk_width],
                global_pairs[..., c0 : c0 + chunk_width],
                extended[..., c0 : c0 + chunk_width],
                chooser, my_slot, my_usable, device, seq_count, capacity,
            )
        )
    query_grads = jnp.concatenate([p[0] for p in pieces], axis=-1)
    totals = jnp.concatenate([p[1] for p in pieces], axis=-1)
    global_sum = jnp.concatenate([p[2] for p in pieces], axis=-1)
    global_sum, totals = lax.optimization_barrier((global_sum, totals))
    everywhere = gather_sum_to_first(global_sum, "seq")
    padded_global = jnp.pad(everywhere, ((0, 0), (0, per_dev - G), (0, 0), (0, 0))) * (
        device == 0
    ).astype(jnp.float32)
    totals = totals + padded_global
    grad_rows = query_grads.reshape(tokens, features).astype(jnp.bfloat16)
    key_rows = totals[0].reshape(tokens, features).astype(jnp.bfloat16)
    value_rows = totals[1].reshape(tokens, features).astype(jnp.bfloat16)
    result = jnp.stack([grad_rows, key_rows, value_rows])
    result = lax.all_to_all(result, "head", split_axis=1, concat_axis=2, tiled=True)
    return (result[0], result[1], result[2])


def solution(mesh):
    in_specs = (
        P(("seq", "head"), None),
        P(("seq", "head"), None),
        P(("seq", "head"), None),
        P(("seq", "head"), None),
        P(),
    )
    out_specs = (P(("seq", "head"), None), P(("seq", "head"), None), P(("seq", "head"), None))
    return jax.shard_map(
        on_device, mesh=mesh, in_specs=in_specs, out_specs=out_specs, check_vma=False
    )
```

```python
import jax
import jax.numpy as jnp
from jax import lax
from jax.sharding import PartitionSpec as P

HD = 128
BLOCK = 64
G = 2
R = 3


big_negative = -1e30


def broadcast(block, axis, source):
    peers = lax.axis_size(axis)
    block = jnp.where(lax.axis_index(axis) == source, block, jnp.zeros_like(block))
    inner = 8 if peers % 8 == 0 else 1
    if inner > 1 and source == 0:
        outer = peers // inner
        received = [
            lax.ppermute(block, axis, [(0, k * inner)]) for k in range(1, outer)
        ]
        for part in received:
            block = block + part
        received = [
            lax.ppermute(block, axis, [(z * inner, z * inner + k) for z in range(outer)])
            for k in range(1, inner)
        ]
        for part in received:
            block = block + part
        return block
    step = 1
    while step * 2 < peers:
        step *= 2
    while step >= 1:
        pairs = [(i, i + step) for i in range(0, peers, 2 * step) if i + step < peers]
        block = block + lax.ppermute(block, axis, pairs)
        step //= 2
    return block


def reduce_to_first(block, axis):
    peers = lax.axis_size(axis)
    step = 1
    while step < peers:
        radix = 4 if peers % (step * 4) == 0 else 2
        received = [
            lax.ppermute(
                block, axis, [(i + k * step, i) for i in range(0, peers, radix * step)]
            )
            for k in range(1, radix)
        ]
        for part in received:
            block = block + part
        step *= radix
    return block


def extended_2(shard, sides, width):
    for axis, dim in sides:
        peers, length = (lax.axis_size(axis), shard.shape[dim])
        up = [(i, (i + 1) % peers) for i in range(peers - 1)]
        down = [(j, i) for i, j in up]
        last = lax.slice_in_dim(shard, length - width, length, axis=dim)
        leading = lax.slice_in_dim(shard, 0, width, axis=dim)
        before = lax.ppermute(last, axis, up)
        after = lax.ppermute(leading, axis, down)
        shard = jnp.concatenate([before, shard, after], axis=dim)
    return shard


def request_plan(requested, device, per_dev):
    wanted_row = requested[device]
    owners = wanted_row // per_dev
    within = wanted_row % per_dev
    usable = jnp.ones(wanted_row.shape, jnp.bool_)
    positions = jnp.arange(owners.shape[0])
    earlier = (owners[:, None] == owners[None, :]) & (positions[None, :] < positions[:, None])
    slot_rank = jnp.sum(earlier.astype(jnp.int32), axis=1)
    return (owners, within, slot_rank, usable)


def attend_chunk(queries, out_grads, own_pairs, outgoing, global_pairs, extended,
                 chooser, my_slot, my_usable, device, seq_count, capacity, after=None):
    tokens, features = queries.shape
    head_count = features // HD
    per_dev = tokens // BLOCK
    rand_count = per_dev * R
    score_scale = HD ** (-0.5)
    incoming = lax.all_to_all(outgoing, "seq", split_axis=0, concat_axis=0, tiled=True)

    left_pair = extended[:, :BLOCK]
    right_pair = extended[:, -BLOCK:]
    framed = jnp.concatenate([left_pair[:, None], own_pairs, right_pair[:, None]], axis=1)
    window = jnp.stack(
        [framed[:, 0:per_dev], framed[:, 1 : per_dev + 1], framed[:, 2 : per_dev + 2]], axis=2
    )
    global_slots = jnp.broadcast_to(global_pairs[:, None], (2, per_dev, G, BLOCK, features))
    local = jnp.concatenate([window, global_slots], axis=2)
    local_count = 3 + G
    local_keys = local[0].reshape(per_dev, local_count, BLOCK, head_count, HD)
    local_values = local[1].reshape(per_dev, local_count, BLOCK, head_count, HD)
    block_index = device * per_dev + jnp.arange(per_dev)
    glob_index = jnp.arange(G)
    intersections = jnp.abs(glob_index[None, :] - block_index[:, None]) <= 1
    live_local = jnp.concatenate(
        [
            (block_index >= 1)[:, None],
            jnp.ones((per_dev, 1), jnp.bool_),
            (block_index <= seq_count * per_dev - 2)[:, None],
            jnp.logical_not(intersections),
        ],
        axis=1,
    )
    query_blocks = queries.reshape(per_dev, BLOCK, head_count, HD)
    dout_blocks = out_grads.reshape(per_dev, BLOCK, head_count, HD)
    scores_local = (
        jnp.einsum("bxhd,bkyhd->bhxky", query_blocks, local_keys, preferred_element_type=jnp.float32)
        * score_scale
    )
    scores_local = jnp.where(live_local[:, None, None, :, None], scores_local, big_negative)
    grads_local = jnp.einsum(
        "bxhd,bkyhd->bhxky", dout_blocks, local_values, preferred_element_type=jnp.float32
    )
    max_local = jnp.max(scores_local, axis=(3, 4), keepdims=True)

    fetched = incoming[my_slot]
    randoms = fetched.reshape(per_dev, R, 2, BLOCK, features)
    rand_keys = randoms[:, :, 0].reshape(per_dev, R, BLOCK, head_count, HD)
    rand_values = randoms[:, :, 1].reshape(per_dev, R, BLOCK, head_count, HD)
    scores_rand = (
        jnp.einsum("bxhd,bkyhd->bhxky", query_blocks, rand_keys, preferred_element_type=jnp.float32)
        * score_scale
    )
    grads_rand = jnp.einsum(
        "bxhd,bkyhd->bhxky", dout_blocks, rand_values, preferred_element_type=jnp.float32
    )
    row_max = jnp.maximum(max_local, jnp.max(scores_rand, axis=(3, 4), keepdims=True))
    weights_local = jnp.exp(scores_local - row_max)
    weights_rand = jnp.exp(scores_rand - row_max)
    row_total = jnp.sum(weights_local, axis=(3, 4), keepdims=True) + jnp.sum(
        weights_rand, axis=(3, 4), keepdims=True
    )
    probs_local = weights_local / row_total
    probs_rand = weights_rand / row_total
    row_dot = jnp.sum(probs_local * grads_local, axis=(3, 4), keepdims=True) + jnp.sum(
        probs_rand * grads_rand, axis=(3, 4), keepdims=True
    )
    dscores_rand = (probs_rand * (grads_rand - row_dot)).astype(jnp.bfloat16)
    low_rand = probs_rand.astype(jnp.bfloat16)
    key_rand = (
        jnp.einsum(
            "bhxky,bxhd->bkyhd", dscores_rand, query_blocks, preferred_element_type=jnp.float32
        )
        * score_scale
    )
    value_rand = jnp.einsum(
        "bhxky,bxhd->bkyhd", low_rand, dout_blocks, preferred_element_type=jnp.float32
    )
    rand_terms = (
        jnp.stack([key_rand, value_rand])
        .reshape(2, rand_count, BLOCK, features)
        .transpose(1, 0, 2, 3)
        .astype(jnp.bfloat16)
    )
    target = jnp.where(my_usable, my_slot, seq_count * capacity)
    placer = (target[:, None] == jnp.arange(seq_count * capacity)[None, :]).astype(jnp.bfloat16)
    outgoing_back = jnp.einsum(
        "js,jkxf->skxf", placer, rand_terms, preferred_element_type=jnp.float32
    ).astype(jnp.bfloat16)
    if after is not None:
        outgoing_back, after = lax.optimization_barrier((outgoing_back, after))
    arrived = lax.all_to_all(outgoing_back, "seq", split_axis=0, concat_axis=0, tiled=True)

    dscores_local = (probs_local * (grads_local - row_dot)).astype(jnp.bfloat16)
    low_local = probs_local.astype(jnp.bfloat16)
    query_grads = (
        jnp.einsum(
            "bhxky,bkyhd->bxhd", dscores_local, local_keys, preferred_element_type=jnp.float32
        )
        + jnp.einsum(
            "bhxky,bkyhd->bxhd", dscores_rand, rand_keys, preferred_element_type=jnp.float32
        )
    ) * score_scale
    key_global = (
        jnp.einsum(
            "bhxky,bxhd->kyhd",
            dscores_local[:, :, :, 3:],
            query_blocks,
            preferred_element_type=jnp.float32,
        )
        * score_scale
    )
    value_global = jnp.einsum(
        "bhxky,bxhd->kyhd", low_local[:, :, :, 3:], dout_blocks, preferred_element_type=jnp.float32
    )
    global_sum = jnp.stack([key_global, value_global]).reshape(2, G, BLOCK, features)
    everywhere = reduce_to_first(global_sum, "seq")
    key_terms = (
        jnp.einsum(
            "bhxky,bxhd->bkyhd",
            dscores_local[:, :, :, :3],
            query_blocks,
            preferred_element_type=jnp.float32,
        )
        * score_scale
    )
    value_terms = jnp.einsum(
        "bhxky,bxhd->bkyhd", low_local[:, :, :, :3], dout_blocks, preferred_element_type=jnp.float32
    )
    pair_terms = jnp.stack([key_terms, value_terms]).reshape(2, per_dev, 3, BLOCK, features)
    framed_sum = jnp.pad(pair_terms[:, :, 0], ((0, 0), (0, 2), (0, 0), (0, 0)))
    framed_sum = framed_sum + jnp.pad(pair_terms[:, :, 1], ((0, 0), (1, 1), (0, 0), (0, 0)))
    framed_sum = framed_sum + jnp.pad(pair_terms[:, :, 2], ((0, 0), (2, 0), (0, 0), (0, 0)))
    totals = framed_sum[:, 1 : per_dev + 1]
    rim_terms = jnp.concatenate([framed_sum[:, 0], framed_sum[:, -1]], axis=1)
    widened = extended_2(rim_terms.astype(jnp.bfloat16), (("seq", 1),), BLOCK).astype(
        rim_terms.dtype
    )
    totals = totals.at[:, 0].add(widened[:, :BLOCK])
    totals = totals.at[:, per_dev - 1].add(widened[:, -BLOCK:])
    padded_global = jnp.pad(everywhere, ((0, 0), (0, per_dev - G), (0, 0), (0, 0))) * (
        device == 0
    ).astype(jnp.float32)
    totals = totals + padded_global
    collected = jnp.einsum(
        "dcb,dcsxf->sbxf",
        chooser.astype(jnp.bfloat16),
        arrived.reshape(seq_count, capacity, 2, BLOCK, features),
        preferred_element_type=jnp.float32,
    )
    totals = totals + collected
    return query_grads.reshape(tokens, features), totals, everywhere


def on_device(query, key, value, grad_out, rand_blocks):
    kv_stacked = jnp.stack([key, value])
    kv_stacked = lax.all_to_all(kv_stacked, "head", split_axis=2, concat_axis=1, tiled=True)
    keys, values = kv_stacked[0], kv_stacked[1]
    qo_stacked = jnp.stack([query, grad_out])
    qo_stacked = lax.all_to_all(qo_stacked, "head", split_axis=2, concat_axis=1, tiled=True)
    queries, out_grads = qo_stacked[0], qo_stacked[1]
    tokens, features = queries.shape
    head_count = features // HD
    per_dev = tokens // BLOCK
    seq_count = lax.axis_size("seq")
    device = lax.axis_index("seq")
    capacity = (per_dev * R + seq_count - 3) // (seq_count - 2)
    rand_count = per_dev * R
    score_scale = HD ** (-0.5)
    requested = rand_blocks.reshape(seq_count, rand_count)
    owners_all, within_all, rank_all, usable_all = jax.vmap(
        lambda sender: request_plan(requested, sender, per_dev)
    )(jnp.arange(seq_count, dtype=jnp.int32))
    to_me = usable_all & (owners_all == device)
    slot_ids = jnp.arange(capacity)
    block_ids = jnp.arange(per_dev)
    matches = (
        to_me[:, :, None, None]
        & (rank_all[:, :, None, None] == slot_ids[None, None, :, None])
        & (within_all[:, :, None, None] == block_ids[None, None, None, :])
    )
    chooser = jnp.sum(matches.astype(jnp.float32), axis=1)
    my_owners, my_within, my_rank, my_usable = request_plan(requested, device, per_dev)
    my_slot = jnp.clip(my_owners, 0, seq_count - 1) * capacity + my_rank
    own_pairs = jnp.stack([keys, values]).reshape(2, per_dev, BLOCK, features)
    served = jnp.einsum(
        "dcb,sbxf->dcsxf",
        chooser.astype(jnp.bfloat16),
        own_pairs,
        preferred_element_type=jnp.float32,
    ).astype(jnp.bfloat16)
    outgoing = served.reshape(seq_count * capacity, 2, BLOCK, features)
    leading = jnp.stack([keys[: G * BLOCK], values[: G * BLOCK]])
    global_pairs = broadcast(leading, "seq", 0).reshape(2, G, BLOCK, features)
    extended = extended_2(jnp.stack([keys, values]), (("seq", 1),), BLOCK)
    outgoing, queries, out_grads, extended = lax.optimization_barrier(
        (outgoing, queries, out_grads, extended)
    )
    chunk_heads = 2 if head_count % 2 == 0 else 1
    chunk_width = chunk_heads * HD
    pieces = []
    for c0 in range(0, features, chunk_width):
        pieces.append(
            attend_chunk(
                queries[:, c0 : c0 + chunk_width],
                out_grads[:, c0 : c0 + chunk_width],
                own_pairs[..., c0 : c0 + chunk_width],
                outgoing[..., c0 : c0 + chunk_width],
                global_pairs[..., c0 : c0 + chunk_width],
                extended[..., c0 : c0 + chunk_width],
                chooser, my_slot, my_usable, device, seq_count, capacity,
            )
        )
    query_grads = jnp.concatenate([p[0] for p in pieces], axis=-1)
    totals = jnp.concatenate([p[1] for p in pieces], axis=-1)
    grad_rows = query_grads.reshape(tokens, features).astype(jnp.bfloat16)
    key_rows = totals[0].reshape(tokens, features).astype(jnp.bfloat16)
    value_rows = totals[1].reshape(tokens, features).astype(jnp.bfloat16)
    result = jnp.stack([grad_rows, key_rows, value_rows])
    result = lax.all_to_all(result, "head", split_axis=1, concat_axis=2, tiled=True)
    return (result[0], result[1], result[2])


def solution(mesh):
    in_specs = (
        P(("seq", "head"), None),
        P(("seq", "head"), None),
        P(("seq", "head"), None),
        P(("seq", "head"), None),
        P(),
    )
    out_specs = (P(("seq", "head"), None), P(("seq", "head"), None), P(("seq", "head"), None))
    return jax.shard_map(
        on_device, mesh=mesh, in_specs=in_specs, out_specs=out_specs, check_vma=False
    )
```

```python
import jax
import jax.numpy as jnp
from jax import lax
from jax.sharding import PartitionSpec as P

HD = 128
BLOCK = 64
G = 2
R = 3


big_negative = -1e30


def broadcast(block, axis, source):
    peers = lax.axis_size(axis)
    block = jnp.where(lax.axis_index(axis) == source, block, jnp.zeros_like(block))
    inner = 8 if peers % 8 == 0 else 1
    if inner > 1 and source == 0:
        outer = peers // inner
        received = [
            lax.ppermute(block, axis, [(0, k * inner)]) for k in range(1, outer)
        ]
        for part in received:
            block = block + part
        received = [
            lax.ppermute(block, axis, [(z * inner, z * inner + k) for z in range(outer)])
            for k in range(1, inner)
        ]
        for part in received:
            block = block + part
        return block
    step = 1
    while step * 2 < peers:
        step *= 2
    while step >= 1:
        pairs = [(i, i + step) for i in range(0, peers, 2 * step) if i + step < peers]
        block = block + lax.ppermute(block, axis, pairs)
        step //= 2
    return block


def reduce_to_first(block, axis):
    peers = lax.axis_size(axis)
    step = 1
    while step < peers:
        radix = 4 if peers % (step * 4) == 0 else 2
        received = [
            lax.ppermute(
                block, axis, [(i + k * step, i) for i in range(0, peers, radix * step)]
            )
            for k in range(1, radix)
        ]
        for part in received:
            block = block + part
        step *= radix
    return block


def extended_2(shard, sides, width):
    for axis, dim in sides:
        peers, length = (lax.axis_size(axis), shard.shape[dim])
        up = [(i, (i + 1) % peers) for i in range(peers - 1)]
        down = [(j, i) for i, j in up]
        last = lax.slice_in_dim(shard, length - width, length, axis=dim)
        leading = lax.slice_in_dim(shard, 0, width, axis=dim)
        before = lax.ppermute(last, axis, up)
        after = lax.ppermute(leading, axis, down)
        shard = jnp.concatenate([before, shard, after], axis=dim)
    return shard


def request_plan(requested, device, per_dev):
    wanted_row = requested[device]
    owners = wanted_row // per_dev
    within = wanted_row % per_dev
    usable = jnp.ones(wanted_row.shape, jnp.bool_)
    positions = jnp.arange(owners.shape[0])
    earlier = (owners[:, None] == owners[None, :]) & (positions[None, :] < positions[:, None])
    slot_rank = jnp.sum(earlier.astype(jnp.int32), axis=1)
    return (owners, within, slot_rank, usable)


def attend_chunk(queries, out_grads, own_pairs, outgoing, global_pairs, extended,
                 chooser, my_slot, my_usable, device, seq_count, capacity, early=False):
    tokens, features = queries.shape
    head_count = features // HD
    per_dev = tokens // BLOCK
    rand_count = per_dev * R
    score_scale = HD ** (-0.5)

    left_pair = extended[:, :BLOCK]
    right_pair = extended[:, -BLOCK:]
    framed = jnp.concatenate([left_pair[:, None], own_pairs, right_pair[:, None]], axis=1)
    window = jnp.stack(
        [framed[:, 0:per_dev], framed[:, 1 : per_dev + 1], framed[:, 2 : per_dev + 2]], axis=2
    )
    global_slots = jnp.broadcast_to(global_pairs[:, None], (2, per_dev, G, BLOCK, features))
    local = jnp.concatenate([window, global_slots], axis=2)
    local_count = 3 + G
    local_keys = local[0].reshape(per_dev, local_count, BLOCK, head_count, HD)
    local_values = local[1].reshape(per_dev, local_count, BLOCK, head_count, HD)
    block_index = device * per_dev + jnp.arange(per_dev)
    glob_index = jnp.arange(G)
    intersections = jnp.abs(glob_index[None, :] - block_index[:, None]) <= 1
    live_local = jnp.concatenate(
        [
            (block_index >= 1)[:, None],
            jnp.ones((per_dev, 1), jnp.bool_),
            (block_index <= seq_count * per_dev - 2)[:, None],
            jnp.logical_not(intersections),
        ],
        axis=1,
    )
    query_blocks = queries.reshape(per_dev, BLOCK, head_count, HD)
    dout_blocks = out_grads.reshape(per_dev, BLOCK, head_count, HD)
    scores_local = (
        jnp.einsum("bxhd,bkyhd->bhxky", query_blocks, local_keys, preferred_element_type=jnp.float32)
        * score_scale
    )
    scores_local = jnp.where(live_local[:, None, None, :, None], scores_local, big_negative)
    grads_local = jnp.einsum(
        "bxhd,bkyhd->bhxky", dout_blocks, local_values, preferred_element_type=jnp.float32
    )
    max_local = jnp.max(scores_local, axis=(3, 4), keepdims=True)

    if early:
        outgoing, scores_local, grads_local, max_local = lax.optimization_barrier(
            (outgoing, scores_local, grads_local, max_local)
        )
    incoming = lax.all_to_all(outgoing, "seq", split_axis=0, concat_axis=0, tiled=True)
    fetched = incoming[my_slot]
    randoms = fetched.reshape(per_dev, R, 2, BLOCK, features)
    rand_keys = randoms[:, :, 0].reshape(per_dev, R, BLOCK, head_count, HD)
    rand_values = randoms[:, :, 1].reshape(per_dev, R, BLOCK, head_count, HD)
    scores_rand = (
        jnp.einsum("bxhd,bkyhd->bhxky", query_blocks, rand_keys, preferred_element_type=jnp.float32)
        * score_scale
    )
    grads_rand = jnp.einsum(
        "bxhd,bkyhd->bhxky", dout_blocks, rand_values, preferred_element_type=jnp.float32
    )
    row_max = jnp.maximum(max_local, jnp.max(scores_rand, axis=(3, 4), keepdims=True))
    weights_local = jnp.exp(scores_local - row_max)
    weights_rand = jnp.exp(scores_rand - row_max)
    row_total = jnp.sum(weights_local, axis=(3, 4), keepdims=True) + jnp.sum(
        weights_rand, axis=(3, 4), keepdims=True
    )
    probs_local = weights_local / row_total
    probs_rand = weights_rand / row_total
    row_dot = jnp.sum(probs_local * grads_local, axis=(3, 4), keepdims=True) + jnp.sum(
        probs_rand * grads_rand, axis=(3, 4), keepdims=True
    )
    dscores_rand = (probs_rand * (grads_rand - row_dot)).astype(jnp.bfloat16)
    low_rand = probs_rand.astype(jnp.bfloat16)
    key_rand = (
        jnp.einsum(
            "bhxky,bxhd->bkyhd", dscores_rand, query_blocks, preferred_element_type=jnp.float32
        )
        * score_scale
    )
    value_rand = jnp.einsum(
        "bhxky,bxhd->bkyhd", low_rand, dout_blocks, preferred_element_type=jnp.float32
    )
    rand_terms = (
        jnp.stack([key_rand, value_rand])
        .reshape(2, rand_count, BLOCK, features)
        .transpose(1, 0, 2, 3)
        .astype(jnp.bfloat16)
    )
    dscores_local = (probs_local * (grads_local - row_dot)).astype(jnp.bfloat16)
    low_local = probs_local.astype(jnp.bfloat16)
    key_global = (
        jnp.einsum(
            "bhxky,bxhd->kyhd",
            dscores_local[:, :, :, 3:],
            query_blocks,
            preferred_element_type=jnp.float32,
        )
        * score_scale
    )
    value_global = jnp.einsum(
        "bhxky,bxhd->kyhd", low_local[:, :, :, 3:], dout_blocks, preferred_element_type=jnp.float32
    )
    halves = jnp.stack([key_global, value_global]).reshape(2, G * BLOCK * features)
    is_even = (device % 2) == 0
    partner = [(i, i ^ 1) for i in range(seq_count)]
    handed = lax.ppermute(jnp.where(is_even, halves[1], halves[0]), "seq", partner)
    kept = jnp.where(is_even, halves[0], halves[1]) + handed
    target = jnp.where(my_usable, my_slot, seq_count * capacity)
    placer = (target[:, None] == jnp.arange(seq_count * capacity)[None, :]).astype(jnp.bfloat16)
    outgoing_back = jnp.einsum(
        "js,jkxf->skxf", placer, rand_terms, preferred_element_type=jnp.float32
    ).astype(jnp.bfloat16)
    outgoing_back = outgoing_back.at[0].set(kept.reshape(2, BLOCK, features).astype(jnp.bfloat16))
    arrived = lax.all_to_all(outgoing_back, "seq", split_axis=0, concat_axis=0, tiled=True)
    firsts = arrived.reshape(seq_count, capacity, G * BLOCK * features)[:, 0].astype(jnp.float32)
    firsts = firsts.reshape(seq_count // 2, 2, G * BLOCK * features)
    everywhere = jnp.sum(firsts, axis=0).reshape(2, G, BLOCK, features)

    query_grads = (
        jnp.einsum(
            "bhxky,bkyhd->bxhd", dscores_local, local_keys, preferred_element_type=jnp.float32
        )
        + jnp.einsum(
            "bhxky,bkyhd->bxhd", dscores_rand, rand_keys, preferred_element_type=jnp.float32
        )
    ) * score_scale
    key_terms = (
        jnp.einsum(
            "bhxky,bxhd->bkyhd",
            dscores_local[:, :, :, :3],
            query_blocks,
            preferred_element_type=jnp.float32,
        )
        * score_scale
    )
    value_terms = jnp.einsum(
        "bhxky,bxhd->bkyhd", low_local[:, :, :, :3], dout_blocks, preferred_element_type=jnp.float32
    )
    pair_terms = jnp.stack([key_terms, value_terms]).reshape(2, per_dev, 3, BLOCK, features)
    framed_sum = jnp.pad(pair_terms[:, :, 0], ((0, 0), (0, 2), (0, 0), (0, 0)))
    framed_sum = framed_sum + jnp.pad(pair_terms[:, :, 1], ((0, 0), (1, 1), (0, 0), (0, 0)))
    framed_sum = framed_sum + jnp.pad(pair_terms[:, :, 2], ((0, 0), (2, 0), (0, 0), (0, 0)))
    totals = framed_sum[:, 1 : per_dev + 1]
    rim_terms = jnp.concatenate([framed_sum[:, 0], framed_sum[:, -1]], axis=1)
    widened = extended_2(rim_terms.astype(jnp.bfloat16), (("seq", 1),), BLOCK).astype(
        rim_terms.dtype
    )
    totals = totals.at[:, 0].add(widened[:, :BLOCK])
    totals = totals.at[:, per_dev - 1].add(widened[:, -BLOCK:])
    padded_global = jnp.pad(everywhere, ((0, 0), (0, per_dev - G), (0, 0), (0, 0))) * (
        device == 0
    ).astype(jnp.float32)
    totals = totals + padded_global
    collected = jnp.einsum(
        "dcb,dcsxf->sbxf",
        chooser.astype(jnp.bfloat16),
        arrived.reshape(seq_count, capacity, 2, BLOCK, features),
        preferred_element_type=jnp.float32,
    )
    totals = totals + collected
    return query_grads.reshape(tokens, features), totals, everywhere


def on_device(query, key, value, grad_out, rand_blocks):
    kv_stacked = jnp.stack([key, value])
    kv_stacked = lax.all_to_all(kv_stacked, "head", split_axis=2, concat_axis=1, tiled=True)
    keys, values = kv_stacked[0], kv_stacked[1]
    qo_stacked = jnp.stack([query, grad_out])
    qo_stacked = lax.all_to_all(qo_stacked, "head", split_axis=2, concat_axis=1, tiled=True)
    queries, out_grads = qo_stacked[0], qo_stacked[1]
    tokens, features = queries.shape
    head_count = features // HD
    per_dev = tokens // BLOCK
    seq_count = lax.axis_size("seq")
    device = lax.axis_index("seq")
    capacity = (per_dev * R + seq_count - 3) // (seq_count - 2)
    rand_count = per_dev * R
    score_scale = HD ** (-0.5)
    requested = rand_blocks.reshape(seq_count, rand_count)
    owners_all, within_all, rank_all, usable_all = jax.vmap(
        lambda sender: request_plan(requested, sender, per_dev)
    )(jnp.arange(seq_count, dtype=jnp.int32))
    to_me = usable_all & (owners_all == device)
    slot_ids = jnp.arange(capacity)
    block_ids = jnp.arange(per_dev)
    matches = (
        to_me[:, :, None, None]
        & (rank_all[:, :, None, None] == slot_ids[None, None, :, None])
        & (within_all[:, :, None, None] == block_ids[None, None, None, :])
    )
    chooser = jnp.sum(matches.astype(jnp.float32), axis=1)
    my_owners, my_within, my_rank, my_usable = request_plan(requested, device, per_dev)
    my_slot = jnp.clip(my_owners, 0, seq_count - 1) * capacity + my_rank
    own_pairs = jnp.stack([keys, values]).reshape(2, per_dev, BLOCK, features)
    served = jnp.einsum(
        "dcb,sbxf->dcsxf",
        chooser.astype(jnp.bfloat16),
        own_pairs,
        preferred_element_type=jnp.float32,
    ).astype(jnp.bfloat16)
    outgoing = served.reshape(seq_count * capacity, 2, BLOCK, features)
    leading = jnp.stack([keys[: G * BLOCK], values[: G * BLOCK]])
    global_pairs = broadcast(leading, "seq", 0).reshape(2, G, BLOCK, features)
    extended = extended_2(jnp.stack([keys, values]), (("seq", 1),), BLOCK)
    outgoing, global_pairs, extended = lax.optimization_barrier((outgoing, global_pairs, extended))
    chunk_heads = 2 if head_count % 2 == 0 else 1
    chunk_width = chunk_heads * HD
    pieces = []
    for c0 in range(0, features, chunk_width):
        pieces.append(
            attend_chunk(
                queries[:, c0 : c0 + chunk_width],
                out_grads[:, c0 : c0 + chunk_width],
                own_pairs[..., c0 : c0 + chunk_width],
                outgoing[..., c0 : c0 + chunk_width],
                global_pairs[..., c0 : c0 + chunk_width],
                extended[..., c0 : c0 + chunk_width],
                chooser, my_slot, my_usable, device, seq_count, capacity,
                early=bool(pieces),
            )
        )
    query_grads = jnp.concatenate([p[0] for p in pieces], axis=-1)
    totals = jnp.concatenate([p[1] for p in pieces], axis=-1)
    grad_rows = query_grads.reshape(tokens, features).astype(jnp.bfloat16)
    key_rows = totals[0].reshape(tokens, features).astype(jnp.bfloat16)
    value_rows = totals[1].reshape(tokens, features).astype(jnp.bfloat16)
    result = jnp.stack([grad_rows, key_rows, value_rows])
    result = lax.all_to_all(result, "head", split_axis=1, concat_axis=2, tiled=True)
    return (result[0], result[1], result[2])


def solution(mesh):
    in_specs = (
        P(("seq", "head"), None),
        P(("seq", "head"), None),
        P(("seq", "head"), None),
        P(("seq", "head"), None),
        P(),
    )
    out_specs = (P(("seq", "head"), None), P(("seq", "head"), None), P(("seq", "head"), None))
    return jax.shard_map(
        on_device, mesh=mesh, in_specs=in_specs, out_specs=out_specs, check_vma=False
    )
```

```python
import jax
import jax.numpy as jnp
from jax import lax
from jax.sharding import PartitionSpec as P

HD = 128
BLOCK = 64
G = 2
R = 3


big_negative = -1e30


def broadcast(block, axis, source):
    peers = lax.axis_size(axis)
    block = jnp.where(lax.axis_index(axis) == source, block, jnp.zeros_like(block))
    inner = 8 if peers % 8 == 0 else 1
    if inner > 1 and source == 0:
        outer = peers // inner
        received = [
            lax.ppermute(block, axis, [(0, k * inner)]) for k in range(1, outer)
        ]
        for part in received:
            block = block + part
        received = [
            lax.ppermute(block, axis, [(z * inner, z * inner + k) for z in range(outer)])
            for k in range(1, inner)
        ]
        for part in received:
            block = block + part
        return block
    step = 1
    while step * 2 < peers:
        step *= 2
    while step >= 1:
        pairs = [(i, i + step) for i in range(0, peers, 2 * step) if i + step < peers]
        block = block + lax.ppermute(block, axis, pairs)
        step //= 2
    return block


def reduce_to_first(block, axis):
    peers = lax.axis_size(axis)
    step = 1
    while step < peers:
        radix = 4 if peers % (step * 4) == 0 else 2
        received = [
            lax.ppermute(
                block, axis, [(i + k * step, i) for i in range(0, peers, radix * step)]
            )
            for k in range(1, radix)
        ]
        for part in received:
            block = block + part
        step *= radix
    return block


def extended_2(shard, sides, width):
    for axis, dim in sides:
        peers, length = (lax.axis_size(axis), shard.shape[dim])
        up = [(i, (i + 1) % peers) for i in range(peers - 1)]
        down = [(j, i) for i, j in up]
        last = lax.slice_in_dim(shard, length - width, length, axis=dim)
        leading = lax.slice_in_dim(shard, 0, width, axis=dim)
        before = lax.ppermute(last, axis, up)
        after = lax.ppermute(leading, axis, down)
        shard = jnp.concatenate([before, shard, after], axis=dim)
    return shard


def request_plan(requested, device, per_dev):
    wanted_row = requested[device]
    owners = wanted_row // per_dev
    within = wanted_row % per_dev
    usable = jnp.ones(wanted_row.shape, jnp.bool_)
    positions = jnp.arange(owners.shape[0])
    earlier = (owners[:, None] == owners[None, :]) & (positions[None, :] < positions[:, None])
    slot_rank = jnp.sum(earlier.astype(jnp.int32), axis=1)
    return (owners, within, slot_rank, usable)


def attend_chunk(queries, out_grads, own_pairs, outgoing, global_pairs, extended,
                 chooser, my_slot, my_usable, device, seq_count, capacity, early=False):
    tokens, features = queries.shape
    head_count = features // HD
    per_dev = tokens // BLOCK
    rand_count = per_dev * R
    score_scale = HD ** (-0.5)

    left_pair = extended[:, :BLOCK]
    right_pair = extended[:, -BLOCK:]
    framed = jnp.concatenate([left_pair[:, None], own_pairs, right_pair[:, None]], axis=1)
    window = jnp.stack(
        [framed[:, 0:per_dev], framed[:, 1 : per_dev + 1], framed[:, 2 : per_dev + 2]], axis=2
    )
    global_slots = jnp.broadcast_to(global_pairs[:, None], (2, per_dev, G, BLOCK, features))
    local = jnp.concatenate([window, global_slots], axis=2)
    local_count = 3 + G
    local_keys = local[0].reshape(per_dev, local_count, BLOCK, head_count, HD)
    local_values = local[1].reshape(per_dev, local_count, BLOCK, head_count, HD)
    block_index = device * per_dev + jnp.arange(per_dev)
    glob_index = jnp.arange(G)
    intersections = jnp.abs(glob_index[None, :] - block_index[:, None]) <= 1
    live_local = jnp.concatenate(
        [
            (block_index >= 1)[:, None],
            jnp.ones((per_dev, 1), jnp.bool_),
            (block_index <= seq_count * per_dev - 2)[:, None],
            jnp.logical_not(intersections),
        ],
        axis=1,
    )
    query_blocks = queries.reshape(per_dev, BLOCK, head_count, HD)
    dout_blocks = out_grads.reshape(per_dev, BLOCK, head_count, HD)
    scores_local = (
        jnp.einsum("bxhd,bkyhd->bhxky", query_blocks, local_keys, preferred_element_type=jnp.float32)
        * score_scale
    )
    scores_local = jnp.where(live_local[:, None, None, :, None], scores_local, big_negative)
    grads_local = jnp.einsum(
        "bxhd,bkyhd->bhxky", dout_blocks, local_values, preferred_element_type=jnp.float32
    )
    max_local = jnp.max(scores_local, axis=(3, 4), keepdims=True)

    if early:
        outgoing, scores_local, grads_local, max_local = lax.optimization_barrier(
            (outgoing, scores_local, grads_local, max_local)
        )
    incoming = lax.all_to_all(outgoing, "seq", split_axis=0, concat_axis=0, tiled=True)
    fetched = incoming[my_slot]
    randoms = fetched.reshape(per_dev, R, 2, BLOCK, features)
    rand_keys = randoms[:, :, 0].reshape(per_dev, R, BLOCK, head_count, HD)
    rand_values = randoms[:, :, 1].reshape(per_dev, R, BLOCK, head_count, HD)
    scores_rand = (
        jnp.einsum("bxhd,bkyhd->bhxky", query_blocks, rand_keys, preferred_element_type=jnp.float32)
        * score_scale
    )
    grads_rand = jnp.einsum(
        "bxhd,bkyhd->bhxky", dout_blocks, rand_values, preferred_element_type=jnp.float32
    )
    row_max = jnp.maximum(max_local, jnp.max(scores_rand, axis=(3, 4), keepdims=True))
    weights_local = jnp.exp(scores_local - row_max)
    weights_rand = jnp.exp(scores_rand - row_max)
    row_total = jnp.sum(weights_local, axis=(3, 4), keepdims=True) + jnp.sum(
        weights_rand, axis=(3, 4), keepdims=True
    )
    probs_local = weights_local / row_total
    probs_rand = weights_rand / row_total
    row_dot = jnp.sum(probs_local * grads_local, axis=(3, 4), keepdims=True) + jnp.sum(
        probs_rand * grads_rand, axis=(3, 4), keepdims=True
    )
    dscores_rand = (probs_rand * (grads_rand - row_dot)).astype(jnp.bfloat16)
    low_rand = probs_rand.astype(jnp.bfloat16)
    key_rand = (
        jnp.einsum(
            "bhxky,bxhd->bkyhd", dscores_rand, query_blocks, preferred_element_type=jnp.float32
        )
        * score_scale
    )
    value_rand = jnp.einsum(
        "bhxky,bxhd->bkyhd", low_rand, dout_blocks, preferred_element_type=jnp.float32
    )
    rand_terms = (
        jnp.stack([key_rand, value_rand])
        .reshape(2, rand_count, BLOCK, features)
        .transpose(1, 0, 2, 3)
        .astype(jnp.bfloat16)
    )
    dscores_local = (probs_local * (grads_local - row_dot)).astype(jnp.bfloat16)
    low_local = probs_local.astype(jnp.bfloat16)
    key_global = (
        jnp.einsum(
            "bhxky,bxhd->kyhd",
            dscores_local[:, :, :, 3:],
            query_blocks,
            preferred_element_type=jnp.float32,
        )
        * score_scale
    )
    value_global = jnp.einsum(
        "bhxky,bxhd->kyhd", low_local[:, :, :, 3:], dout_blocks, preferred_element_type=jnp.float32
    )
    halves = jnp.stack([key_global, value_global]).reshape(2, G * BLOCK * features)
    is_even = (device % 2) == 0
    partner = [(i, i ^ 1) for i in range(seq_count)]
    handed = lax.ppermute(jnp.where(is_even, halves[1], halves[0]), "seq", partner)
    kept = jnp.where(is_even, halves[0], halves[1]) + handed
    target = jnp.where(my_usable, my_slot, seq_count * capacity)
    placer = (target[:, None] == jnp.arange(seq_count * capacity)[None, :]).astype(jnp.bfloat16)
    outgoing_back = jnp.einsum(
        "js,jkxf->skxf", placer, rand_terms, preferred_element_type=jnp.float32
    ).astype(jnp.bfloat16)
    outgoing_back = outgoing_back.at[0].set(kept.reshape(2, BLOCK, features).astype(jnp.bfloat16))
    arrived = lax.all_to_all(outgoing_back, "seq", split_axis=0, concat_axis=0, tiled=True)
    firsts = arrived.reshape(seq_count, capacity, G * BLOCK * features)[:, 0].astype(jnp.float32)
    firsts = firsts.reshape(seq_count // 2, 2, G * BLOCK * features)
    everywhere = jnp.sum(firsts, axis=0).reshape(2, G, BLOCK, features)

    query_grads = (
        jnp.einsum(
            "bhxky,bkyhd->bxhd", dscores_local, local_keys, preferred_element_type=jnp.float32
        )
        + jnp.einsum(
            "bhxky,bkyhd->bxhd", dscores_rand, rand_keys, preferred_element_type=jnp.float32
        )
    ) * score_scale
    key_terms = (
        jnp.einsum(
            "bhxky,bxhd->bkyhd",
            dscores_local[:, :, :, :3],
            query_blocks,
            preferred_element_type=jnp.float32,
        )
        * score_scale
    )
    value_terms = jnp.einsum(
        "bhxky,bxhd->bkyhd", low_local[:, :, :, :3], dout_blocks, preferred_element_type=jnp.float32
    )
    pair_terms = jnp.stack([key_terms, value_terms]).reshape(2, per_dev, 3, BLOCK, features)
    framed_sum = jnp.pad(pair_terms[:, :, 0], ((0, 0), (0, 2), (0, 0), (0, 0)))
    framed_sum = framed_sum + jnp.pad(pair_terms[:, :, 1], ((0, 0), (1, 1), (0, 0), (0, 0)))
    framed_sum = framed_sum + jnp.pad(pair_terms[:, :, 2], ((0, 0), (2, 0), (0, 0), (0, 0)))
    totals = framed_sum[:, 1 : per_dev + 1]
    rim_terms = jnp.concatenate([framed_sum[:, 0], framed_sum[:, -1]], axis=1)
    padded_global = jnp.pad(everywhere, ((0, 0), (0, per_dev - G), (0, 0), (0, 0))) * (
        device == 0
    ).astype(jnp.float32)
    totals = totals + padded_global
    collected = jnp.einsum(
        "dcb,dcsxf->sbxf",
        chooser.astype(jnp.bfloat16),
        arrived.reshape(seq_count, capacity, 2, BLOCK, features),
        preferred_element_type=jnp.float32,
    )
    totals = totals + collected
    return query_grads.reshape(tokens, features), totals, rim_terms


def on_device(query, key, value, grad_out, rand_blocks):
    kv_stacked = jnp.stack([key, value])
    kv_stacked = lax.all_to_all(kv_stacked, "head", split_axis=2, concat_axis=1, tiled=True)
    keys, values = kv_stacked[0], kv_stacked[1]
    qo_stacked = jnp.stack([query, grad_out])
    qo_stacked = lax.all_to_all(qo_stacked, "head", split_axis=2, concat_axis=1, tiled=True)
    queries, out_grads = qo_stacked[0], qo_stacked[1]
    tokens, features = queries.shape
    head_count = features // HD
    per_dev = tokens // BLOCK
    seq_count = lax.axis_size("seq")
    device = lax.axis_index("seq")
    capacity = (per_dev * R + seq_count - 3) // (seq_count - 2)
    rand_count = per_dev * R
    score_scale = HD ** (-0.5)
    requested = rand_blocks.reshape(seq_count, rand_count)
    owners_all, within_all, rank_all, usable_all = jax.vmap(
        lambda sender: request_plan(requested, sender, per_dev)
    )(jnp.arange(seq_count, dtype=jnp.int32))
    to_me = usable_all & (owners_all == device)
    slot_ids = jnp.arange(capacity)
    block_ids = jnp.arange(per_dev)
    matches = (
        to_me[:, :, None, None]
        & (rank_all[:, :, None, None] == slot_ids[None, None, :, None])
        & (within_all[:, :, None, None] == block_ids[None, None, None, :])
    )
    chooser = jnp.sum(matches.astype(jnp.float32), axis=1)
    my_owners, my_within, my_rank, my_usable = request_plan(requested, device, per_dev)
    my_slot = jnp.clip(my_owners, 0, seq_count - 1) * capacity + my_rank
    own_pairs = jnp.stack([keys, values]).reshape(2, per_dev, BLOCK, features)
    served = jnp.einsum(
        "dcb,sbxf->dcsxf",
        chooser.astype(jnp.bfloat16),
        own_pairs,
        preferred_element_type=jnp.float32,
    ).astype(jnp.bfloat16)
    outgoing = served.reshape(seq_count * capacity, 2, BLOCK, features)
    leading = jnp.stack([keys[: G * BLOCK], values[: G * BLOCK]])
    global_pairs = broadcast(leading, "seq", 0).reshape(2, G, BLOCK, features)
    extended = extended_2(jnp.stack([keys, values]), (("seq", 1),), BLOCK)
    outgoing, global_pairs, extended = lax.optimization_barrier((outgoing, global_pairs, extended))
    chunk_heads = 2 if head_count % 2 == 0 else 1
    chunk_width = chunk_heads * HD
    pieces = []
    for c0 in range(0, features, chunk_width):
        pieces.append(
            attend_chunk(
                queries[:, c0 : c0 + chunk_width],
                out_grads[:, c0 : c0 + chunk_width],
                own_pairs[..., c0 : c0 + chunk_width],
                outgoing[..., c0 : c0 + chunk_width],
                global_pairs[..., c0 : c0 + chunk_width],
                extended[..., c0 : c0 + chunk_width],
                chooser, my_slot, my_usable, device, seq_count, capacity,
                early=bool(pieces),
            )
        )
    query_grads = jnp.concatenate([p[0] for p in pieces], axis=-1)
    totals = jnp.concatenate([p[1] for p in pieces], axis=-1)
    rim_terms = jnp.concatenate([p[2] for p in pieces], axis=-1)
    rim_terms, totals = lax.optimization_barrier((rim_terms, totals))
    widened = extended_2(rim_terms.astype(jnp.bfloat16), (("seq", 1),), BLOCK).astype(
        rim_terms.dtype
    )
    totals = totals.at[:, 0].add(widened[:, :BLOCK])
    totals = totals.at[:, per_dev - 1].add(widened[:, -BLOCK:])
    grad_rows = query_grads.reshape(tokens, features).astype(jnp.bfloat16)
    key_rows = totals[0].reshape(tokens, features).astype(jnp.bfloat16)
    value_rows = totals[1].reshape(tokens, features).astype(jnp.bfloat16)
    result = jnp.stack([grad_rows, key_rows, value_rows])
    result = lax.all_to_all(result, "head", split_axis=1, concat_axis=2, tiled=True)
    return (result[0], result[1], result[2])


def solution(mesh):
    in_specs = (
        P(("seq", "head"), None),
        P(("seq", "head"), None),
        P(("seq", "head"), None),
        P(("seq", "head"), None),
        P(),
    )
    out_specs = (P(("seq", "head"), None), P(("seq", "head"), None), P(("seq", "head"), None))
    return jax.shard_map(
        on_device, mesh=mesh, in_specs=in_specs, out_specs=out_specs, check_vma=False
    )
```

```python
import jax
import jax.numpy as jnp
from jax import lax
from jax.sharding import PartitionSpec as P

HD = 128
BLOCK = 64
G = 2
R = 3


big_negative = -1e30


def broadcast(block, axis, source):
    peers = lax.axis_size(axis)
    block = jnp.where(lax.axis_index(axis) == source, block, jnp.zeros_like(block))
    inner = 8 if peers % 8 == 0 else 1
    if inner > 1 and source == 0:
        outer = peers // inner
        received = [
            lax.ppermute(block, axis, [(0, k * inner)]) for k in range(1, outer)
        ]
        for part in received:
            block = block + part
        received = [
            lax.ppermute(block, axis, [(z * inner, z * inner + k) for z in range(outer)])
            for k in range(1, inner)
        ]
        for part in received:
            block = block + part
        return block
    step = 1
    while step * 2 < peers:
        step *= 2
    while step >= 1:
        pairs = [(i, i + step) for i in range(0, peers, 2 * step) if i + step < peers]
        block = block + lax.ppermute(block, axis, pairs)
        step //= 2
    return block


def reduce_to_first(block, axis):
    peers = lax.axis_size(axis)
    step = 1
    while step < peers:
        radix = 4 if peers % (step * 4) == 0 else 2
        received = [
            lax.ppermute(
                block, axis, [(i + k * step, i) for i in range(0, peers, radix * step)]
            )
            for k in range(1, radix)
        ]
        for part in received:
            block = block + part
        step *= radix
    return block


def extended_2(shard, sides, width):
    for axis, dim in sides:
        peers, length = (lax.axis_size(axis), shard.shape[dim])
        up = [(i, (i + 1) % peers) for i in range(peers - 1)]
        down = [(j, i) for i, j in up]
        last = lax.slice_in_dim(shard, length - width, length, axis=dim)
        leading = lax.slice_in_dim(shard, 0, width, axis=dim)
        before = lax.ppermute(last, axis, up)
        after = lax.ppermute(leading, axis, down)
        shard = jnp.concatenate([before, shard, after], axis=dim)
    return shard


def request_plan(requested, device, per_dev):
    wanted_row = requested[device]
    owners = wanted_row // per_dev
    within = wanted_row % per_dev
    usable = jnp.ones(wanted_row.shape, jnp.bool_)
    positions = jnp.arange(owners.shape[0])
    earlier = (owners[:, None] == owners[None, :]) & (positions[None, :] < positions[:, None])
    slot_rank = jnp.sum(earlier.astype(jnp.int32), axis=1)
    return (owners, within, slot_rank, usable)


def local_chunk(queries, out_grads, own_pairs, global_pairs, extended, device, seq_count):
    tokens, features = queries.shape
    head_count = features // HD
    per_dev = tokens // BLOCK
    score_scale = HD ** (-0.5)

    left_pair = extended[:, :BLOCK]
    right_pair = extended[:, -BLOCK:]
    framed = jnp.concatenate([left_pair[:, None], own_pairs, right_pair[:, None]], axis=1)
    window = jnp.stack(
        [framed[:, 0:per_dev], framed[:, 1 : per_dev + 1], framed[:, 2 : per_dev + 2]], axis=2
    )
    global_slots = jnp.broadcast_to(global_pairs[:, None], (2, per_dev, G, BLOCK, features))
    local = jnp.concatenate([window, global_slots], axis=2)
    local_count = 3 + G
    local_keys = local[0].reshape(per_dev, local_count, BLOCK, head_count, HD)
    local_values = local[1].reshape(per_dev, local_count, BLOCK, head_count, HD)
    block_index = device * per_dev + jnp.arange(per_dev)
    glob_index = jnp.arange(G)
    intersections = jnp.abs(glob_index[None, :] - block_index[:, None]) <= 1
    live_local = jnp.concatenate(
        [
            (block_index >= 1)[:, None],
            jnp.ones((per_dev, 1), jnp.bool_),
            (block_index <= seq_count * per_dev - 2)[:, None],
            jnp.logical_not(intersections),
        ],
        axis=1,
    )
    query_blocks = queries.reshape(per_dev, BLOCK, head_count, HD)
    dout_blocks = out_grads.reshape(per_dev, BLOCK, head_count, HD)
    scores_local = (
        jnp.einsum("bxhd,bkyhd->bhxky", query_blocks, local_keys, preferred_element_type=jnp.float32)
        * score_scale
    )
    scores_local = jnp.where(live_local[:, None, None, :, None], scores_local, big_negative)
    grads_local = jnp.einsum(
        "bxhd,bkyhd->bhxky", dout_blocks, local_values, preferred_element_type=jnp.float32
    )
    max_local = jnp.max(scores_local, axis=(3, 4), keepdims=True)
    return (local_keys, local_values, query_blocks, dout_blocks, scores_local, grads_local, max_local)


def attend_chunk(queries, outgoing, state, chooser, my_slot, my_usable, device, seq_count,
                 capacity, hold=()):
    tokens, features = queries.shape
    head_count = features // HD
    per_dev = tokens // BLOCK
    rand_count = per_dev * R
    score_scale = HD ** (-0.5)
    local_keys, local_values, query_blocks, dout_blocks, scores_local, grads_local, max_local = state
    incoming = lax.all_to_all(outgoing, "seq", split_axis=0, concat_axis=0, tiled=True)
    if hold:
        incoming, hold = lax.optimization_barrier((incoming, hold))
    fetched = incoming[my_slot]
    randoms = fetched.reshape(per_dev, R, 2, BLOCK, features)
    rand_keys = randoms[:, :, 0].reshape(per_dev, R, BLOCK, head_count, HD)
    rand_values = randoms[:, :, 1].reshape(per_dev, R, BLOCK, head_count, HD)
    scores_rand = (
        jnp.einsum("bxhd,bkyhd->bhxky", query_blocks, rand_keys, preferred_element_type=jnp.float32)
        * score_scale
    )
    grads_rand = jnp.einsum(
        "bxhd,bkyhd->bhxky", dout_blocks, rand_values, preferred_element_type=jnp.float32
    )
    row_max = jnp.maximum(max_local, jnp.max(scores_rand, axis=(3, 4), keepdims=True))
    weights_local = jnp.exp(scores_local - row_max)
    weights_rand = jnp.exp(scores_rand - row_max)
    row_total = jnp.sum(weights_local, axis=(3, 4), keepdims=True) + jnp.sum(
        weights_rand, axis=(3, 4), keepdims=True
    )
    probs_local = weights_local / row_total
    probs_rand = weights_rand / row_total
    row_dot = jnp.sum(probs_local * grads_local, axis=(3, 4), keepdims=True) + jnp.sum(
        probs_rand * grads_rand, axis=(3, 4), keepdims=True
    )
    dscores_rand = (probs_rand * (grads_rand - row_dot)).astype(jnp.bfloat16)
    low_rand = probs_rand.astype(jnp.bfloat16)
    key_rand = (
        jnp.einsum(
            "bhxky,bxhd->bkyhd", dscores_rand, query_blocks, preferred_element_type=jnp.float32
        )
        * score_scale
    )
    value_rand = jnp.einsum(
        "bhxky,bxhd->bkyhd", low_rand, dout_blocks, preferred_element_type=jnp.float32
    )
    rand_terms = (
        jnp.stack([key_rand, value_rand])
        .reshape(2, rand_count, BLOCK, features)
        .transpose(1, 0, 2, 3)
        .astype(jnp.bfloat16)
    )
    dscores_local = (probs_local * (grads_local - row_dot)).astype(jnp.bfloat16)
    low_local = probs_local.astype(jnp.bfloat16)
    key_global = (
        jnp.einsum(
            "bhxky,bxhd->kyhd",
            dscores_local[:, :, :, 3:],
            query_blocks,
            preferred_element_type=jnp.float32,
        )
        * score_scale
    )
    value_global = jnp.einsum(
        "bhxky,bxhd->kyhd", low_local[:, :, :, 3:], dout_blocks, preferred_element_type=jnp.float32
    )
    halves = jnp.stack([key_global, value_global]).reshape(2, G * BLOCK * features)
    is_even = (device % 2) == 0
    partner = [(i, i ^ 1) for i in range(seq_count)]
    handed = lax.ppermute(jnp.where(is_even, halves[1], halves[0]), "seq", partner)
    kept = jnp.where(is_even, halves[0], halves[1]) + handed
    target = jnp.where(my_usable, my_slot, seq_count * capacity)
    placer = (target[:, None] == jnp.arange(seq_count * capacity)[None, :]).astype(jnp.bfloat16)
    outgoing_back = jnp.einsum(
        "js,jkxf->skxf", placer, rand_terms, preferred_element_type=jnp.float32
    ).astype(jnp.bfloat16)
    outgoing_back = outgoing_back.at[0].set(kept.reshape(2, BLOCK, features).astype(jnp.bfloat16))
    arrived = lax.all_to_all(outgoing_back, "seq", split_axis=0, concat_axis=0, tiled=True)
    firsts = arrived.reshape(seq_count, capacity, G * BLOCK * features)[:, 0].astype(jnp.float32)
    firsts = firsts.reshape(seq_count // 2, 2, G * BLOCK * features)
    everywhere = jnp.sum(firsts, axis=0).reshape(2, G, BLOCK, features)

    query_grads = (
        jnp.einsum(
            "bhxky,bkyhd->bxhd", dscores_local, local_keys, preferred_element_type=jnp.float32
        )
        + jnp.einsum(
            "bhxky,bkyhd->bxhd", dscores_rand, rand_keys, preferred_element_type=jnp.float32
        )
    ) * score_scale
    key_terms = (
        jnp.einsum(
            "bhxky,bxhd->bkyhd",
            dscores_local[:, :, :, :3],
            query_blocks,
            preferred_element_type=jnp.float32,
        )
        * score_scale
    )
    value_terms = jnp.einsum(
        "bhxky,bxhd->bkyhd", low_local[:, :, :, :3], dout_blocks, preferred_element_type=jnp.float32
    )
    pair_terms = jnp.stack([key_terms, value_terms]).reshape(2, per_dev, 3, BLOCK, features)
    framed_sum = jnp.pad(pair_terms[:, :, 0], ((0, 0), (0, 2), (0, 0), (0, 0)))
    framed_sum = framed_sum + jnp.pad(pair_terms[:, :, 1], ((0, 0), (1, 1), (0, 0), (0, 0)))
    framed_sum = framed_sum + jnp.pad(pair_terms[:, :, 2], ((0, 0), (2, 0), (0, 0), (0, 0)))
    totals = framed_sum[:, 1 : per_dev + 1]
    rim_terms = jnp.concatenate([framed_sum[:, 0], framed_sum[:, -1]], axis=1)
    padded_global = jnp.pad(everywhere, ((0, 0), (0, per_dev - G), (0, 0), (0, 0))) * (
        device == 0
    ).astype(jnp.float32)
    totals = totals + padded_global
    collected = jnp.einsum(
        "dcb,dcsxf->sbxf",
        chooser.astype(jnp.bfloat16),
        arrived.reshape(seq_count, capacity, 2, BLOCK, features),
        preferred_element_type=jnp.float32,
    )
    totals = totals + collected
    return query_grads.reshape(tokens, features), totals, rim_terms, hold


def on_device(query, key, value, grad_out, rand_blocks):
    kv_stacked = jnp.stack([key, value])
    kv_stacked = lax.all_to_all(kv_stacked, "head", split_axis=2, concat_axis=1, tiled=True)
    keys, values = kv_stacked[0], kv_stacked[1]
    qo_stacked = jnp.stack([query, grad_out])
    qo_stacked = lax.all_to_all(qo_stacked, "head", split_axis=2, concat_axis=1, tiled=True)
    queries, out_grads = qo_stacked[0], qo_stacked[1]
    tokens, features = queries.shape
    head_count = features // HD
    per_dev = tokens // BLOCK
    seq_count = lax.axis_size("seq")
    device = lax.axis_index("seq")
    capacity = (per_dev * R + seq_count - 3) // (seq_count - 2)
    rand_count = per_dev * R
    score_scale = HD ** (-0.5)
    requested = rand_blocks.reshape(seq_count, rand_count)
    owners_all, within_all, rank_all, usable_all = jax.vmap(
        lambda sender: request_plan(requested, sender, per_dev)
    )(jnp.arange(seq_count, dtype=jnp.int32))
    to_me = usable_all & (owners_all == device)
    slot_ids = jnp.arange(capacity)
    block_ids = jnp.arange(per_dev)
    matches = (
        to_me[:, :, None, None]
        & (rank_all[:, :, None, None] == slot_ids[None, None, :, None])
        & (within_all[:, :, None, None] == block_ids[None, None, None, :])
    )
    chooser = jnp.sum(matches.astype(jnp.float32), axis=1)
    my_owners, my_within, my_rank, my_usable = request_plan(requested, device, per_dev)
    my_slot = jnp.clip(my_owners, 0, seq_count - 1) * capacity + my_rank
    own_pairs = jnp.stack([keys, values]).reshape(2, per_dev, BLOCK, features)
    served = jnp.einsum(
        "dcb,sbxf->dcsxf",
        chooser.astype(jnp.bfloat16),
        own_pairs,
        preferred_element_type=jnp.float32,
    ).astype(jnp.bfloat16)
    outgoing = served.reshape(seq_count * capacity, 2, BLOCK, features)
    leading = jnp.stack([keys[: G * BLOCK], values[: G * BLOCK]])
    global_pairs = broadcast(leading, "seq", 0).reshape(2, G, BLOCK, features)
    extended = extended_2(jnp.stack([keys, values]), (("seq", 1),), BLOCK)
    outgoing, global_pairs, extended = lax.optimization_barrier((outgoing, global_pairs, extended))
    chunk_heads = 2 if head_count % 2 == 0 else 1
    chunk_width = chunk_heads * HD
    states = [
        local_chunk(
            queries[:, c0 : c0 + chunk_width],
            out_grads[:, c0 : c0 + chunk_width],
            own_pairs[..., c0 : c0 + chunk_width],
            global_pairs[..., c0 : c0 + chunk_width],
            extended[..., c0 : c0 + chunk_width],
            device,
            seq_count,
        )
        for c0 in range(0, features, chunk_width)
    ]
    pieces = []
    held = ()
    for index, c0 in enumerate(range(0, features, chunk_width)):
        state = states[index] if index == 0 else held[index - 1]
        piece = attend_chunk(
            queries[:, c0 : c0 + chunk_width],
            outgoing[..., c0 : c0 + chunk_width],
            state, chooser, my_slot, my_usable, device, seq_count, capacity,
            hold=tuple(states[1:]) if index == 0 else (),
        )
        if index == 0:
            held = piece[3]
        pieces.append(piece)
    query_grads = jnp.concatenate([p[0] for p in pieces], axis=-1)
    totals = jnp.concatenate([p[1] for p in pieces], axis=-1)
    rim_terms = jnp.concatenate([p[2] for p in pieces], axis=-1)
    rim_terms, totals = lax.optimization_barrier((rim_terms, totals))
    widened = extended_2(rim_terms.astype(jnp.bfloat16), (("seq", 1),), BLOCK).astype(
        rim_terms.dtype
    )
    totals = totals.at[:, 0].add(widened[:, :BLOCK])
    totals = totals.at[:, per_dev - 1].add(widened[:, -BLOCK:])
    grad_rows = query_grads.reshape(tokens, features).astype(jnp.bfloat16)
    key_rows = totals[0].reshape(tokens, features).astype(jnp.bfloat16)
    value_rows = totals[1].reshape(tokens, features).astype(jnp.bfloat16)
    result = jnp.stack([grad_rows, key_rows, value_rows])
    result = lax.all_to_all(result, "head", split_axis=1, concat_axis=2, tiled=True)
    return (result[0], result[1], result[2])


def solution(mesh):
    in_specs = (
        P(("seq", "head"), None),
        P(("seq", "head"), None),
        P(("seq", "head"), None),
        P(("seq", "head"), None),
        P(),
    )
    out_specs = (P(("seq", "head"), None), P(("seq", "head"), None), P(("seq", "head"), None))
    return jax.shard_map(
        on_device, mesh=mesh, in_specs=in_specs, out_specs=out_specs, check_vma=False
    )
```

```python
import jax
import jax.numpy as jnp
from jax import lax
from jax.sharding import PartitionSpec as P

HD = 128
BLOCK = 64
G = 2
R = 3


big_negative = -1e30


def broadcast(block, axis, source):
    peers = lax.axis_size(axis)
    block = jnp.where(lax.axis_index(axis) == source, block, jnp.zeros_like(block))
    inner = 8 if peers % 8 == 0 else 1
    if inner > 1 and source == 0:
        outer = peers // inner
        received = [
            lax.ppermute(block, axis, [(0, k * inner)]) for k in range(1, outer)
        ]
        for part in received:
            block = block + part
        received = [
            lax.ppermute(block, axis, [(z * inner, z * inner + k) for z in range(outer)])
            for k in range(1, inner)
        ]
        for part in received:
            block = block + part
        return block
    step = 1
    while step * 2 < peers:
        step *= 2
    while step >= 1:
        pairs = [(i, i + step) for i in range(0, peers, 2 * step) if i + step < peers]
        block = block + lax.ppermute(block, axis, pairs)
        step //= 2
    return block


def reduce_to_first(block, axis):
    peers = lax.axis_size(axis)
    step = 1
    while step < peers:
        radix = 4 if peers % (step * 4) == 0 else 2
        received = [
            lax.ppermute(
                block, axis, [(i + k * step, i) for i in range(0, peers, radix * step)]
            )
            for k in range(1, radix)
        ]
        for part in received:
            block = block + part
        step *= radix
    return block


def extended_2(shard, sides, width):
    for axis, dim in sides:
        peers, length = (lax.axis_size(axis), shard.shape[dim])
        up = [(i, (i + 1) % peers) for i in range(peers - 1)]
        down = [(j, i) for i, j in up]
        last = lax.slice_in_dim(shard, length - width, length, axis=dim)
        leading = lax.slice_in_dim(shard, 0, width, axis=dim)
        before = lax.ppermute(last, axis, up)
        after = lax.ppermute(leading, axis, down)
        shard = jnp.concatenate([before, shard, after], axis=dim)
    return shard


def request_plan(requested, device, per_dev):
    wanted_row = requested[device]
    owners = wanted_row // per_dev
    within = wanted_row % per_dev
    usable = jnp.ones(wanted_row.shape, jnp.bool_)
    positions = jnp.arange(owners.shape[0])
    earlier = (owners[:, None] == owners[None, :]) & (positions[None, :] < positions[:, None])
    slot_rank = jnp.sum(earlier.astype(jnp.int32), axis=1)
    return (owners, within, slot_rank, usable)


def local_chunk(queries, out_grads, own_pairs, global_pairs, extended, device, seq_count):
    tokens, features = queries.shape
    head_count = features // HD
    per_dev = tokens // BLOCK
    score_scale = HD ** (-0.5)

    left_pair = extended[:, :BLOCK]
    right_pair = extended[:, -BLOCK:]
    framed = jnp.concatenate([left_pair[:, None], own_pairs, right_pair[:, None]], axis=1)
    window = jnp.stack(
        [framed[:, 0:per_dev], framed[:, 1 : per_dev + 1], framed[:, 2 : per_dev + 2]], axis=2
    )
    global_slots = jnp.broadcast_to(global_pairs[:, None], (2, per_dev, G, BLOCK, features))
    local = jnp.concatenate([window, global_slots], axis=2)
    local_count = 3 + G
    local_keys = local[0].reshape(per_dev, local_count, BLOCK, head_count, HD)
    local_values = local[1].reshape(per_dev, local_count, BLOCK, head_count, HD)
    block_index = device * per_dev + jnp.arange(per_dev)
    glob_index = jnp.arange(G)
    intersections = jnp.abs(glob_index[None, :] - block_index[:, None]) <= 1
    live_local = jnp.concatenate(
        [
            (block_index >= 1)[:, None],
            jnp.ones((per_dev, 1), jnp.bool_),
            (block_index <= seq_count * per_dev - 2)[:, None],
            jnp.logical_not(intersections),
        ],
        axis=1,
    )
    query_blocks = queries.reshape(per_dev, BLOCK, head_count, HD)
    dout_blocks = out_grads.reshape(per_dev, BLOCK, head_count, HD)
    scores_local = (
        jnp.einsum("bxhd,bkyhd->bhxky", query_blocks, local_keys, preferred_element_type=jnp.float32)
        * score_scale
    )
    scores_local = jnp.where(live_local[:, None, None, :, None], scores_local, big_negative)
    grads_local = jnp.einsum(
        "bxhd,bkyhd->bhxky", dout_blocks, local_values, preferred_element_type=jnp.float32
    )
    max_local = jnp.max(scores_local, axis=(3, 4), keepdims=True)
    return (local_keys, local_values, query_blocks, dout_blocks, scores_local, grads_local, max_local)


def attend_chunk(queries, outgoing, state, chooser, my_slot, my_usable, device, seq_count,
                 capacity, hold=()):
    tokens, features = queries.shape
    head_count = features // HD
    per_dev = tokens // BLOCK
    rand_count = per_dev * R
    score_scale = HD ** (-0.5)
    local_keys, local_values, query_blocks, dout_blocks, scores_local, grads_local, max_local = state
    incoming = lax.all_to_all(outgoing, "seq", split_axis=0, concat_axis=0, tiled=True)
    if hold:
        incoming, hold = lax.optimization_barrier((incoming, hold))
    fetched = incoming[my_slot]
    randoms = fetched.reshape(per_dev, R, 2, BLOCK, features)
    rand_keys = randoms[:, :, 0].reshape(per_dev, R, BLOCK, head_count, HD)
    rand_values = randoms[:, :, 1].reshape(per_dev, R, BLOCK, head_count, HD)
    scores_rand = (
        jnp.einsum("bxhd,bkyhd->bhxky", query_blocks, rand_keys, preferred_element_type=jnp.float32)
        * score_scale
    )
    grads_rand = jnp.einsum(
        "bxhd,bkyhd->bhxky", dout_blocks, rand_values, preferred_element_type=jnp.float32
    )
    row_max = jnp.maximum(max_local, jnp.max(scores_rand, axis=(3, 4), keepdims=True))
    weights_local = jnp.exp(scores_local - row_max)
    weights_rand = jnp.exp(scores_rand - row_max)
    row_total = jnp.sum(weights_local, axis=(3, 4), keepdims=True) + jnp.sum(
        weights_rand, axis=(3, 4), keepdims=True
    )
    probs_local = weights_local / row_total
    probs_rand = weights_rand / row_total
    row_dot = jnp.sum(probs_local * grads_local, axis=(3, 4), keepdims=True) + jnp.sum(
        probs_rand * grads_rand, axis=(3, 4), keepdims=True
    )
    dscores_rand = (probs_rand * (grads_rand - row_dot)).astype(jnp.bfloat16)
    low_rand = probs_rand.astype(jnp.bfloat16)
    key_rand = (
        jnp.einsum(
            "bhxky,bxhd->bkyhd", dscores_rand, query_blocks, preferred_element_type=jnp.float32
        )
        * score_scale
    )
    value_rand = jnp.einsum(
        "bhxky,bxhd->bkyhd", low_rand, dout_blocks, preferred_element_type=jnp.float32
    )
    rand_terms = (
        jnp.stack([key_rand, value_rand])
        .reshape(2, rand_count, BLOCK, features)
        .transpose(1, 0, 2, 3)
        .astype(jnp.bfloat16)
    )
    dscores_local = (probs_local * (grads_local - row_dot)).astype(jnp.bfloat16)
    low_local = probs_local.astype(jnp.bfloat16)
    key_global = (
        jnp.einsum(
            "bhxky,bxhd->kyhd",
            dscores_local[:, :, :, 3:],
            query_blocks,
            preferred_element_type=jnp.float32,
        )
        * score_scale
    )
    value_global = jnp.einsum(
        "bhxky,bxhd->kyhd", low_local[:, :, :, 3:], dout_blocks, preferred_element_type=jnp.float32
    )
    halves = jnp.stack([key_global, value_global]).reshape(2, G, BLOCK, features)
    is_even = (device % 2) == 0
    partner = [(i, i ^ 1) for i in range(seq_count)]
    handed = lax.ppermute(jnp.where(is_even, halves[1], halves[0]), "seq", partner)
    kept = jnp.where(is_even, halves[0], halves[1]) + handed
    target = jnp.where(my_usable, my_slot, seq_count * capacity)
    placer = (target[:, None] == jnp.arange(seq_count * capacity)[None, :]).astype(jnp.bfloat16)
    outgoing_back = jnp.einsum(
        "js,jkxf->skxf", placer, rand_terms, preferred_element_type=jnp.float32
    ).astype(jnp.bfloat16)
    outgoing_back = outgoing_back.at[0].set(kept.astype(jnp.bfloat16))
    arrived = lax.all_to_all(outgoing_back, "seq", split_axis=0, concat_axis=0, tiled=True)
    firsts = arrived.reshape(seq_count, capacity, 2, BLOCK, features)[:, 0]
    firsts = firsts.reshape(seq_count // 2, 2, G, BLOCK, features)
    everywhere = jnp.sum(firsts.astype(jnp.float32), axis=0)

    query_grads = (
        jnp.einsum(
            "bhxky,bkyhd->bxhd", dscores_local, local_keys, preferred_element_type=jnp.float32
        )
        + jnp.einsum(
            "bhxky,bkyhd->bxhd", dscores_rand, rand_keys, preferred_element_type=jnp.float32
        )
    ) * score_scale
    key_terms = (
        jnp.einsum(
            "bhxky,bxhd->bkyhd",
            dscores_local[:, :, :, :3],
            query_blocks,
            preferred_element_type=jnp.float32,
        )
        * score_scale
    )
    value_terms = jnp.einsum(
        "bhxky,bxhd->bkyhd", low_local[:, :, :, :3], dout_blocks, preferred_element_type=jnp.float32
    )
    pair_terms = jnp.stack([key_terms, value_terms]).reshape(2, per_dev, 3, BLOCK, features)
    framed_sum = jnp.pad(pair_terms[:, :, 0], ((0, 0), (0, 2), (0, 0), (0, 0)))
    framed_sum = framed_sum + jnp.pad(pair_terms[:, :, 1], ((0, 0), (1, 1), (0, 0), (0, 0)))
    framed_sum = framed_sum + jnp.pad(pair_terms[:, :, 2], ((0, 0), (2, 0), (0, 0), (0, 0)))
    totals = framed_sum[:, 1 : per_dev + 1]
    rim_terms = jnp.concatenate([framed_sum[:, 0], framed_sum[:, -1]], axis=1)
    padded_global = jnp.pad(everywhere, ((0, 0), (0, per_dev - G), (0, 0), (0, 0))) * (
        device == 0
    ).astype(jnp.float32)
    totals = totals + padded_global
    collected = jnp.einsum(
        "dcb,dcsxf->sbxf",
        chooser.astype(jnp.bfloat16),
        arrived.reshape(seq_count, capacity, 2, BLOCK, features),
        preferred_element_type=jnp.float32,
    )
    totals = totals + collected
    return query_grads.reshape(tokens, features), totals, rim_terms, hold


def on_device(query, key, value, grad_out, rand_blocks):
    kv_stacked = jnp.stack([key, value])
    kv_stacked = lax.all_to_all(kv_stacked, "head", split_axis=2, concat_axis=1, tiled=True)
    keys, values = kv_stacked[0], kv_stacked[1]
    qo_stacked = jnp.stack([query, grad_out])
    qo_stacked = lax.all_to_all(qo_stacked, "head", split_axis=2, concat_axis=1, tiled=True)
    queries, out_grads = qo_stacked[0], qo_stacked[1]
    tokens, features = queries.shape
    head_count = features // HD
    per_dev = tokens // BLOCK
    seq_count = lax.axis_size("seq")
    device = lax.axis_index("seq")
    capacity = (per_dev * R + seq_count - 3) // (seq_count - 2)
    rand_count = per_dev * R
    score_scale = HD ** (-0.5)
    requested = rand_blocks.reshape(seq_count, rand_count)
    owners_all, within_all, rank_all, usable_all = jax.vmap(
        lambda sender: request_plan(requested, sender, per_dev)
    )(jnp.arange(seq_count, dtype=jnp.int32))
    to_me = usable_all & (owners_all == device)
    slot_ids = jnp.arange(capacity)
    block_ids = jnp.arange(per_dev)
    matches = (
        to_me[:, :, None, None]
        & (rank_all[:, :, None, None] == slot_ids[None, None, :, None])
        & (within_all[:, :, None, None] == block_ids[None, None, None, :])
    )
    chooser = jnp.sum(matches.astype(jnp.float32), axis=1)
    my_owners, my_within, my_rank, my_usable = request_plan(requested, device, per_dev)
    my_slot = jnp.clip(my_owners, 0, seq_count - 1) * capacity + my_rank
    own_pairs = jnp.stack([keys, values]).reshape(2, per_dev, BLOCK, features)
    served = jnp.einsum(
        "dcb,sbxf->dcsxf",
        chooser.astype(jnp.bfloat16),
        own_pairs,
        preferred_element_type=jnp.float32,
    ).astype(jnp.bfloat16)
    outgoing = served.reshape(seq_count * capacity, 2, BLOCK, features)
    leading = jnp.stack([keys[: G * BLOCK], values[: G * BLOCK]])
    global_pairs = broadcast(leading, "seq", 0).reshape(2, G, BLOCK, features)
    extended = extended_2(jnp.stack([keys, values]), (("seq", 1),), BLOCK)
    outgoing, global_pairs, extended = lax.optimization_barrier((outgoing, global_pairs, extended))
    chunk_heads = 2 if head_count % 2 == 0 else 1
    chunk_width = chunk_heads * HD
    states = [
        local_chunk(
            queries[:, c0 : c0 + chunk_width],
            out_grads[:, c0 : c0 + chunk_width],
            own_pairs[..., c0 : c0 + chunk_width],
            global_pairs[..., c0 : c0 + chunk_width],
            extended[..., c0 : c0 + chunk_width],
            device,
            seq_count,
        )
        for c0 in range(0, features, chunk_width)
    ]
    pieces = []
    held = ()
    for index, c0 in enumerate(range(0, features, chunk_width)):
        state = states[index] if index == 0 else held[index - 1]
        piece = attend_chunk(
            queries[:, c0 : c0 + chunk_width],
            outgoing[..., c0 : c0 + chunk_width],
            state, chooser, my_slot, my_usable, device, seq_count, capacity,
            hold=tuple(states[1:]) if index == 0 else (),
        )
        if index == 0:
            held = piece[3]
        pieces.append(piece)
    query_grads = jnp.concatenate([p[0] for p in pieces], axis=-1)
    totals = jnp.concatenate([p[1] for p in pieces], axis=-1)
    rim_terms = jnp.concatenate([p[2] for p in pieces], axis=-1)
    rim_terms, totals = lax.optimization_barrier((rim_terms, totals))
    widened = extended_2(rim_terms.astype(jnp.bfloat16), (("seq", 1),), BLOCK).astype(
        rim_terms.dtype
    )
    totals = totals.at[:, 0].add(widened[:, :BLOCK])
    totals = totals.at[:, per_dev - 1].add(widened[:, -BLOCK:])
    grad_rows = query_grads.reshape(tokens, features).astype(jnp.bfloat16)
    key_rows = totals[0].reshape(tokens, features).astype(jnp.bfloat16)
    value_rows = totals[1].reshape(tokens, features).astype(jnp.bfloat16)
    result = jnp.stack([grad_rows, key_rows, value_rows])
    result = lax.all_to_all(result, "head", split_axis=1, concat_axis=2, tiled=True)
    return (result[0], result[1], result[2])


def solution(mesh):
    in_specs = (
        P(("seq", "head"), None),
        P(("seq", "head"), None),
        P(("seq", "head"), None),
        P(("seq", "head"), None),
        P(),
    )
    out_specs = (P(("seq", "head"), None), P(("seq", "head"), None), P(("seq", "head"), None))
    return jax.shard_map(
        on_device, mesh=mesh, in_specs=in_specs, out_specs=out_specs, check_vma=False
    )
```

```python
import jax
import jax.numpy as jnp
from jax import lax
from jax.sharding import PartitionSpec as P

HD = 128
BLOCK = 64
G = 2
R = 3


big_negative = -1e30


def broadcast(block, axis, source):
    peers = lax.axis_size(axis)
    block = jnp.where(lax.axis_index(axis) == source, block, jnp.zeros_like(block))
    inner = 8 if peers % 8 == 0 else 1
    if inner > 1 and source == 0:
        outer = peers // inner
        received = [
            lax.ppermute(block, axis, [(0, k * inner)]) for k in range(1, outer)
        ]
        for part in received:
            block = block + part
        received = [
            lax.ppermute(block, axis, [(z * inner, z * inner + k) for z in range(outer)])
            for k in range(1, inner)
        ]
        for part in received:
            block = block + part
        return block
    step = 1
    while step * 2 < peers:
        step *= 2
    while step >= 1:
        pairs = [(i, i + step) for i in range(0, peers, 2 * step) if i + step < peers]
        block = block + lax.ppermute(block, axis, pairs)
        step //= 2
    return block


def reduce_to_first(block, axis):
    peers = lax.axis_size(axis)
    step = 1
    while step < peers:
        radix = 4 if peers % (step * 4) == 0 else 2
        received = [
            lax.ppermute(
                block, axis, [(i + k * step, i) for i in range(0, peers, radix * step)]
            )
            for k in range(1, radix)
        ]
        for part in received:
            block = block + part
        step *= radix
    return block


def extended_2(shard, sides, width):
    for axis, dim in sides:
        peers, length = (lax.axis_size(axis), shard.shape[dim])
        up = [(i, (i + 1) % peers) for i in range(peers - 1)]
        down = [(j, i) for i, j in up]
        last = lax.slice_in_dim(shard, length - width, length, axis=dim)
        leading = lax.slice_in_dim(shard, 0, width, axis=dim)
        before = lax.ppermute(last, axis, up)
        after = lax.ppermute(leading, axis, down)
        shard = jnp.concatenate([before, shard, after], axis=dim)
    return shard


def request_plan(requested, device, per_dev):
    wanted_row = requested[device]
    owners = wanted_row // per_dev
    within = wanted_row % per_dev
    usable = jnp.ones(wanted_row.shape, jnp.bool_)
    positions = jnp.arange(owners.shape[0])
    earlier = (owners[:, None] == owners[None, :]) & (positions[None, :] < positions[:, None])
    slot_rank = jnp.sum(earlier.astype(jnp.int32), axis=1)
    return (owners, within, slot_rank, usable)


def local_chunk(queries, out_grads, own_pairs, global_pairs, extended, device, seq_count):
    tokens, features = queries.shape
    head_count = features // HD
    per_dev = tokens // BLOCK
    score_scale = HD ** (-0.5)

    left_pair = extended[:, :BLOCK]
    right_pair = extended[:, -BLOCK:]
    framed = jnp.concatenate([left_pair[:, None], own_pairs, right_pair[:, None]], axis=1)
    window = jnp.stack(
        [framed[:, 0:per_dev], framed[:, 1 : per_dev + 1], framed[:, 2 : per_dev + 2]], axis=2
    )
    global_slots = jnp.broadcast_to(global_pairs[:, None], (2, per_dev, G, BLOCK, features))
    local = jnp.concatenate([window, global_slots], axis=2)
    local_count = 3 + G
    local_keys = local[0].reshape(per_dev, local_count, BLOCK, head_count, HD)
    local_values = local[1].reshape(per_dev, local_count, BLOCK, head_count, HD)
    block_index = device * per_dev + jnp.arange(per_dev)
    glob_index = jnp.arange(G)
    intersections = jnp.abs(glob_index[None, :] - block_index[:, None]) <= 1
    live_local = jnp.concatenate(
        [
            (block_index >= 1)[:, None],
            jnp.ones((per_dev, 1), jnp.bool_),
            (block_index <= seq_count * per_dev - 2)[:, None],
            jnp.logical_not(intersections),
        ],
        axis=1,
    )
    query_blocks = queries.reshape(per_dev, BLOCK, head_count, HD)
    dout_blocks = out_grads.reshape(per_dev, BLOCK, head_count, HD)
    scores_local = (
        jnp.einsum("bxhd,bkyhd->bhxky", query_blocks, local_keys, preferred_element_type=jnp.float32)
        * score_scale
    )
    scores_local = jnp.where(live_local[:, None, None, :, None], scores_local, big_negative)
    grads_local = jnp.einsum(
        "bxhd,bkyhd->bhxky", dout_blocks, local_values, preferred_element_type=jnp.float32
    )
    max_local = jnp.max(scores_local, axis=(3, 4), keepdims=True)
    return (local_keys, local_values, query_blocks, dout_blocks, scores_local, grads_local, max_local)


def attend_chunk(queries, outgoing, state, chooser, my_slot, my_usable, device, seq_count,
                 capacity, hold=()):
    tokens, features = queries.shape
    head_count = features // HD
    per_dev = tokens // BLOCK
    rand_count = per_dev * R
    score_scale = HD ** (-0.5)
    local_keys, local_values, query_blocks, dout_blocks, scores_local, grads_local, max_local = state
    incoming = lax.all_to_all(outgoing, "seq", split_axis=0, concat_axis=0, tiled=True)
    if hold:
        incoming, hold = lax.optimization_barrier((incoming, hold))
    fetched = incoming[my_slot]
    randoms = fetched.reshape(per_dev, R, 2, BLOCK, features)
    rand_keys = randoms[:, :, 0].reshape(per_dev, R, BLOCK, head_count, HD)
    rand_values = randoms[:, :, 1].reshape(per_dev, R, BLOCK, head_count, HD)
    scores_rand = (
        jnp.einsum("bxhd,bkyhd->bhxky", query_blocks, rand_keys, preferred_element_type=jnp.float32)
        * score_scale
    )
    grads_rand = jnp.einsum(
        "bxhd,bkyhd->bhxky", dout_blocks, rand_values, preferred_element_type=jnp.float32
    )
    row_max = jnp.maximum(max_local, jnp.max(scores_rand, axis=(3, 4), keepdims=True))
    weights_local = jnp.exp(scores_local - row_max)
    weights_rand = jnp.exp(scores_rand - row_max)
    row_total = jnp.sum(weights_local, axis=(3, 4), keepdims=True) + jnp.sum(
        weights_rand, axis=(3, 4), keepdims=True
    )
    probs_local = weights_local / row_total
    probs_rand = weights_rand / row_total
    row_dot = jnp.sum(probs_local * grads_local, axis=(3, 4), keepdims=True) + jnp.sum(
        probs_rand * grads_rand, axis=(3, 4), keepdims=True
    )
    dscores_rand = (probs_rand * (grads_rand - row_dot)).astype(jnp.bfloat16)
    low_rand = probs_rand.astype(jnp.bfloat16)
    key_rand = (
        jnp.einsum(
            "bhxky,bxhd->bkyhd", dscores_rand, query_blocks, preferred_element_type=jnp.float32
        )
        * score_scale
    )
    value_rand = jnp.einsum(
        "bhxky,bxhd->bkyhd", low_rand, dout_blocks, preferred_element_type=jnp.float32
    )
    rand_terms = (
        jnp.stack([key_rand, value_rand])
        .reshape(2, rand_count, BLOCK, features)
        .transpose(1, 0, 2, 3)
        .astype(jnp.bfloat16)
    )
    dscores_local = (probs_local * (grads_local - row_dot)).astype(jnp.bfloat16)
    low_local = probs_local.astype(jnp.bfloat16)
    key_global = (
        jnp.einsum(
            "bhxky,bxhd->kyhd",
            dscores_local[:, :, :, 3:],
            query_blocks,
            preferred_element_type=jnp.float32,
        )
        * score_scale
    )
    value_global = jnp.einsum(
        "bhxky,bxhd->kyhd", low_local[:, :, :, 3:], dout_blocks, preferred_element_type=jnp.float32
    )
    halves = jnp.stack([key_global, value_global]).reshape(2, G, BLOCK, features)
    is_even = (device % 2) == 0
    partner = [(i, i ^ 1) for i in range(seq_count)]
    handed = lax.ppermute(jnp.where(is_even, halves[1], halves[0]), "seq", partner)
    kept = jnp.where(is_even, halves[0], halves[1]) + handed
    target = jnp.where(my_usable, my_slot, seq_count * capacity)
    placer = (target[:, None] == jnp.arange(seq_count * capacity)[None, :]).astype(jnp.bfloat16)
    outgoing_back = jnp.einsum(
        "js,jkxf->skxf", placer, rand_terms, preferred_element_type=jnp.float32
    ).astype(jnp.bfloat16)
    outgoing_back = outgoing_back.at[0].set(kept.astype(jnp.bfloat16))
    arrived = lax.all_to_all(outgoing_back, "seq", split_axis=0, concat_axis=0, tiled=True)
    firsts = arrived.reshape(seq_count, capacity, 2, BLOCK, features)[:, 0]
    firsts = firsts.reshape(seq_count // 2, 2, G, BLOCK, features)
    everywhere = jnp.sum(firsts.astype(jnp.float32), axis=0)

    query_grads = (
        jnp.einsum(
            "bhxky,bkyhd->bxhd", dscores_local, local_keys, preferred_element_type=jnp.float32
        )
        + jnp.einsum(
            "bhxky,bkyhd->bxhd", dscores_rand, rand_keys, preferred_element_type=jnp.float32
        )
    ) * score_scale
    key_terms = (
        jnp.einsum(
            "bhxky,bxhd->bkyhd",
            dscores_local[:, :, :, :3],
            query_blocks,
            preferred_element_type=jnp.float32,
        )
        * score_scale
    )
    value_terms = jnp.einsum(
        "bhxky,bxhd->bkyhd", low_local[:, :, :, :3], dout_blocks, preferred_element_type=jnp.float32
    )
    pair_terms = jnp.stack([key_terms, value_terms]).reshape(2, per_dev, 3, BLOCK, features)
    framed_sum = jnp.pad(pair_terms[:, :, 0], ((0, 0), (0, 2), (0, 0), (0, 0)))
    framed_sum = framed_sum + jnp.pad(pair_terms[:, :, 1], ((0, 0), (1, 1), (0, 0), (0, 0)))
    framed_sum = framed_sum + jnp.pad(pair_terms[:, :, 2], ((0, 0), (2, 0), (0, 0), (0, 0)))
    totals = framed_sum[:, 1 : per_dev + 1]
    rim_terms = jnp.concatenate([framed_sum[:, 0], framed_sum[:, -1]], axis=1)
    padded_global = jnp.pad(everywhere, ((0, 0), (0, per_dev - G), (0, 0), (0, 0))) * (
        device == 0
    ).astype(jnp.float32)
    totals = totals + padded_global
    collected = jnp.einsum(
        "dcb,dcsxf->sbxf",
        chooser.astype(jnp.bfloat16),
        arrived.reshape(seq_count, capacity, 2, BLOCK, features),
        preferred_element_type=jnp.float32,
    )
    totals = totals + collected
    return query_grads.reshape(tokens, features), totals, rim_terms, hold


def on_device(query, key, value, grad_out, rand_blocks):
    kv_stacked = jnp.stack([key, value])
    kv_stacked = lax.all_to_all(kv_stacked, "head", split_axis=2, concat_axis=1, tiled=True)
    keys, values = kv_stacked[0], kv_stacked[1]
    qo_stacked = jnp.stack([query, grad_out])
    qo_stacked = lax.all_to_all(qo_stacked, "head", split_axis=2, concat_axis=1, tiled=True)
    queries, out_grads = qo_stacked[0], qo_stacked[1]
    tokens, features = queries.shape
    head_count = features // HD
    per_dev = tokens // BLOCK
    seq_count = lax.axis_size("seq")
    device = lax.axis_index("seq")
    capacity = (per_dev * R + seq_count - 3) // (seq_count - 2)
    rand_count = per_dev * R
    score_scale = HD ** (-0.5)
    requested = rand_blocks.reshape(seq_count, rand_count)
    owners_all, within_all, rank_all, usable_all = jax.vmap(
        lambda sender: request_plan(requested, sender, per_dev)
    )(jnp.arange(seq_count, dtype=jnp.int32))
    to_me = usable_all & (owners_all == device)
    slot_ids = jnp.arange(capacity)
    block_ids = jnp.arange(per_dev)
    matches = (
        to_me[:, :, None, None]
        & (rank_all[:, :, None, None] == slot_ids[None, None, :, None])
        & (within_all[:, :, None, None] == block_ids[None, None, None, :])
    )
    chooser = jnp.sum(matches.astype(jnp.float32), axis=1)
    my_owners, my_within, my_rank, my_usable = request_plan(requested, device, per_dev)
    my_slot = jnp.clip(my_owners, 0, seq_count - 1) * capacity + my_rank
    own_pairs = jnp.stack([keys, values]).reshape(2, per_dev, BLOCK, features)
    served = jnp.einsum(
        "dcb,sbxf->dcsxf",
        chooser.astype(jnp.bfloat16),
        own_pairs,
        preferred_element_type=jnp.float32,
    ).astype(jnp.bfloat16)
    outgoing = served.reshape(seq_count * capacity, 2, BLOCK, features)
    leading = jnp.stack([keys[: G * BLOCK], values[: G * BLOCK]])
    global_pairs = broadcast(leading, "seq", 0).reshape(2, G, BLOCK, features)
    extended = extended_2(jnp.stack([keys, values]), (("seq", 1),), BLOCK)
    outgoing, global_pairs, extended = lax.optimization_barrier((outgoing, global_pairs, extended))
    chunk_heads = 2 if head_count % 2 == 0 else 1
    chunk_width = chunk_heads * HD
    states = [
        local_chunk(
            queries[:, c0 : c0 + chunk_width],
            out_grads[:, c0 : c0 + chunk_width],
            own_pairs[..., c0 : c0 + chunk_width],
            global_pairs[..., c0 : c0 + chunk_width],
            extended[..., c0 : c0 + chunk_width],
            device,
            seq_count,
        )
        for c0 in range(0, features, chunk_width)
    ]
    pieces = []
    held = ()
    for index, c0 in enumerate(range(0, features, chunk_width)):
        state = states[index] if index == 0 else held[index - 1]
        piece = attend_chunk(
            queries[:, c0 : c0 + chunk_width],
            outgoing[..., c0 : c0 + chunk_width],
            state, chooser, my_slot, my_usable, device, seq_count, capacity,
            hold=tuple(states[1:]) if index == 0 else (),
        )
        if index == 0:
            held = piece[3]
        pieces.append(piece)
    query_grads = jnp.concatenate([p[0] for p in pieces], axis=-1)
    totals = jnp.concatenate([p[1] for p in pieces], axis=-1)
    rim_terms = jnp.concatenate([p[2] for p in pieces], axis=-1)
    rim_terms, totals = lax.optimization_barrier((rim_terms, totals))
    widened = extended_2(rim_terms.astype(jnp.bfloat16), (("seq", 1),), BLOCK).astype(
        rim_terms.dtype
    )
    edges = jnp.concatenate(
        [
            widened[:, None, :BLOCK],
            jnp.zeros((2, per_dev - 2, BLOCK, features), widened.dtype),
            widened[:, None, -BLOCK:],
        ],
        axis=1,
    )
    totals = totals + edges
    grad_rows = query_grads.reshape(tokens, features).astype(jnp.bfloat16)
    key_rows = totals[0].reshape(tokens, features).astype(jnp.bfloat16)
    value_rows = totals[1].reshape(tokens, features).astype(jnp.bfloat16)
    result = jnp.stack([grad_rows, key_rows, value_rows])
    result = lax.all_to_all(result, "head", split_axis=1, concat_axis=2, tiled=True)
    return (result[0], result[1], result[2])


def solution(mesh):
    in_specs = (
        P(("seq", "head"), None),
        P(("seq", "head"), None),
        P(("seq", "head"), None),
        P(("seq", "head"), None),
        P(),
    )
    out_specs = (P(("seq", "head"), None), P(("seq", "head"), None), P(("seq", "head"), None))
    return jax.shard_map(
        on_device, mesh=mesh, in_specs=in_specs, out_specs=out_specs, check_vma=False
    )
```

```python
import jax
import jax.numpy as jnp
from jax import lax
from jax.sharding import PartitionSpec as P

HD = 128
BLOCK = 64
G = 2
R = 3


big_negative = -1e30


def broadcast(block, axis, source):
    peers = lax.axis_size(axis)
    block = jnp.where(lax.axis_index(axis) == source, block, jnp.zeros_like(block))
    inner = 8 if peers % 8 == 0 else 1
    if inner > 1 and source == 0:
        outer = peers // inner
        received = [
            lax.ppermute(block, axis, [(0, k * inner)]) for k in range(1, outer)
        ]
        for part in received:
            block = block + part
        received = [
            lax.ppermute(block, axis, [(z * inner, z * inner + k) for z in range(outer)])
            for k in range(1, inner)
        ]
        for part in received:
            block = block + part
        return block
    step = 1
    while step * 2 < peers:
        step *= 2
    while step >= 1:
        pairs = [(i, i + step) for i in range(0, peers, 2 * step) if i + step < peers]
        block = block + lax.ppermute(block, axis, pairs)
        step //= 2
    return block


def reduce_to_first(block, axis):
    peers = lax.axis_size(axis)
    step = 1
    while step < peers:
        radix = 4 if peers % (step * 4) == 0 else 2
        received = [
            lax.ppermute(
                block, axis, [(i + k * step, i) for i in range(0, peers, radix * step)]
            )
            for k in range(1, radix)
        ]
        for part in received:
            block = block + part
        step *= radix
    return block


def extended_2(shard, sides, width):
    for axis, dim in sides:
        peers, length = (lax.axis_size(axis), shard.shape[dim])
        up = [(i, (i + 1) % peers) for i in range(peers - 1)]
        down = [(j, i) for i, j in up]
        last = lax.slice_in_dim(shard, length - width, length, axis=dim)
        leading = lax.slice_in_dim(shard, 0, width, axis=dim)
        before = lax.ppermute(last, axis, up)
        after = lax.ppermute(leading, axis, down)
        shard = jnp.concatenate([before, shard, after], axis=dim)
    return shard


def request_plan(requested, device, per_dev):
    wanted_row = requested[device]
    owners = wanted_row // per_dev
    within = wanted_row % per_dev
    usable = jnp.ones(wanted_row.shape, jnp.bool_)
    positions = jnp.arange(owners.shape[0])
    earlier = (owners[:, None] == owners[None, :]) & (positions[None, :] < positions[:, None])
    slot_rank = jnp.sum(earlier.astype(jnp.int32), axis=1)
    return (owners, within, slot_rank, usable)


def local_chunk(queries, out_grads, own_pairs, global_pairs, extended, device, seq_count):
    tokens, features = queries.shape
    head_count = features // HD
    per_dev = tokens // BLOCK
    score_scale = HD ** (-0.5)

    left_pair = extended[:, :BLOCK]
    right_pair = extended[:, -BLOCK:]
    framed = jnp.concatenate([left_pair[:, None], own_pairs, right_pair[:, None]], axis=1)
    window = jnp.stack(
        [framed[:, 0:per_dev], framed[:, 1 : per_dev + 1], framed[:, 2 : per_dev + 2]], axis=2
    )
    global_slots = jnp.broadcast_to(global_pairs[:, None], (2, per_dev, G, BLOCK, features))
    local = jnp.concatenate([window, global_slots], axis=2)
    local_count = 3 + G
    local_keys = local[0].reshape(per_dev, local_count, BLOCK, head_count, HD)
    local_values = local[1].reshape(per_dev, local_count, BLOCK, head_count, HD)
    block_index = device * per_dev + jnp.arange(per_dev)
    glob_index = jnp.arange(G)
    intersections = jnp.abs(glob_index[None, :] - block_index[:, None]) <= 1
    live_local = jnp.concatenate(
        [
            (block_index >= 1)[:, None],
            jnp.ones((per_dev, 1), jnp.bool_),
            (block_index <= seq_count * per_dev - 2)[:, None],
            jnp.logical_not(intersections),
        ],
        axis=1,
    )
    query_blocks = queries.reshape(per_dev, BLOCK, head_count, HD)
    dout_blocks = out_grads.reshape(per_dev, BLOCK, head_count, HD)
    scores_local = (
        jnp.einsum("bxhd,bkyhd->bhxky", query_blocks, local_keys, preferred_element_type=jnp.float32)
        * score_scale
    )
    scores_local = jnp.where(live_local[:, None, None, :, None], scores_local, big_negative)
    grads_local = jnp.einsum(
        "bxhd,bkyhd->bhxky", dout_blocks, local_values, preferred_element_type=jnp.float32
    )
    max_local = jnp.max(scores_local, axis=(3, 4), keepdims=True)
    return (local_keys, local_values, query_blocks, dout_blocks, scores_local, grads_local, max_local)


def attend_chunk(queries, outgoing, state, chooser, my_slot, my_usable, device, seq_count,
                 capacity, hold=()):
    tokens, features = queries.shape
    head_count = features // HD
    per_dev = tokens // BLOCK
    rand_count = per_dev * R
    score_scale = HD ** (-0.5)
    local_keys, local_values, query_blocks, dout_blocks, scores_local, grads_local, max_local = state
    incoming = lax.all_to_all(outgoing, "seq", split_axis=0, concat_axis=0, tiled=True)
    if hold:
        incoming, hold = lax.optimization_barrier((incoming, hold))
    fetched = incoming[my_slot]
    randoms = fetched.reshape(per_dev, R, 2, BLOCK, features)
    rand_keys = randoms[:, :, 0].reshape(per_dev, R, BLOCK, head_count, HD)
    rand_values = randoms[:, :, 1].reshape(per_dev, R, BLOCK, head_count, HD)
    scores_rand = (
        jnp.einsum("bxhd,bkyhd->bhxky", query_blocks, rand_keys, preferred_element_type=jnp.float32)
        * score_scale
    )
    grads_rand = jnp.einsum(
        "bxhd,bkyhd->bhxky", dout_blocks, rand_values, preferred_element_type=jnp.float32
    )
    row_max = jnp.maximum(max_local, jnp.max(scores_rand, axis=(3, 4), keepdims=True))
    weights_local = jnp.exp(scores_local - row_max)
    weights_rand = jnp.exp(scores_rand - row_max)
    row_total = jnp.sum(weights_local, axis=(3, 4), keepdims=True) + jnp.sum(
        weights_rand, axis=(3, 4), keepdims=True
    )
    probs_local = weights_local / row_total
    probs_rand = weights_rand / row_total
    row_dot = jnp.sum(probs_local * grads_local, axis=(3, 4), keepdims=True) + jnp.sum(
        probs_rand * grads_rand, axis=(3, 4), keepdims=True
    )
    dscores_rand = (probs_rand * (grads_rand - row_dot)).astype(jnp.bfloat16)
    low_rand = probs_rand.astype(jnp.bfloat16)
    key_rand = (
        jnp.einsum(
            "bhxky,bxhd->bkyhd", dscores_rand, query_blocks, preferred_element_type=jnp.float32
        )
        * score_scale
    )
    value_rand = jnp.einsum(
        "bhxky,bxhd->bkyhd", low_rand, dout_blocks, preferred_element_type=jnp.float32
    )
    rand_terms = (
        jnp.stack([key_rand, value_rand])
        .reshape(2, rand_count, BLOCK, features)
        .transpose(1, 0, 2, 3)
        .astype(jnp.bfloat16)
    )
    dscores_local = (probs_local * (grads_local - row_dot)).astype(jnp.bfloat16)
    low_local = probs_local.astype(jnp.bfloat16)
    key_global = (
        jnp.einsum(
            "bhxky,bxhd->kyhd",
            dscores_local[:, :, :, 3:],
            query_blocks,
            preferred_element_type=jnp.float32,
        )
        * score_scale
    )
    value_global = jnp.einsum(
        "bhxky,bxhd->kyhd", low_local[:, :, :, 3:], dout_blocks, preferred_element_type=jnp.float32
    )
    halves = jnp.stack([key_global, value_global]).reshape(2, G, BLOCK, features)
    is_even = (device % 2) == 0
    partner = [(i, i ^ 1) for i in range(seq_count)]
    handed = lax.ppermute(jnp.where(is_even, halves[1], halves[0]), "seq", partner)
    kept = jnp.where(is_even, halves[0], halves[1]) + handed
    target = jnp.where(my_usable, my_slot, seq_count * capacity)
    placer = (target[:, None] == jnp.arange(seq_count * capacity)[None, :]).astype(jnp.bfloat16)
    outgoing_back = jnp.einsum(
        "js,jkxf->skxf", placer, rand_terms, preferred_element_type=jnp.float32
    ).astype(jnp.bfloat16)
    outgoing_back = jnp.concatenate([kept[None].astype(jnp.bfloat16), outgoing_back[1:]], axis=0)
    arrived = lax.all_to_all(outgoing_back, "seq", split_axis=0, concat_axis=0, tiled=True)
    firsts = arrived.reshape(seq_count, capacity, 2, BLOCK, features)[:, 0]
    firsts = firsts.reshape(seq_count // 2, 2, G, BLOCK, features)
    everywhere = jnp.sum(firsts.astype(jnp.float32), axis=0)

    query_grads = (
        jnp.einsum(
            "bhxky,bkyhd->bxhd", dscores_local, local_keys, preferred_element_type=jnp.float32
        )
        + jnp.einsum(
            "bhxky,bkyhd->bxhd", dscores_rand, rand_keys, preferred_element_type=jnp.float32
        )
    ) * score_scale
    key_terms = (
        jnp.einsum(
            "bhxky,bxhd->bkyhd",
            dscores_local[:, :, :, :3],
            query_blocks,
            preferred_element_type=jnp.float32,
        )
        * score_scale
    )
    value_terms = jnp.einsum(
        "bhxky,bxhd->bkyhd", low_local[:, :, :, :3], dout_blocks, preferred_element_type=jnp.float32
    )
    pair_terms = jnp.stack([key_terms, value_terms]).reshape(2, per_dev, 3, BLOCK, features)
    framed_sum = jnp.pad(pair_terms[:, :, 0], ((0, 0), (0, 2), (0, 0), (0, 0)))
    framed_sum = framed_sum + jnp.pad(pair_terms[:, :, 1], ((0, 0), (1, 1), (0, 0), (0, 0)))
    framed_sum = framed_sum + jnp.pad(pair_terms[:, :, 2], ((0, 0), (2, 0), (0, 0), (0, 0)))
    totals = framed_sum[:, 1 : per_dev + 1]
    rim_terms = jnp.concatenate([framed_sum[:, 0], framed_sum[:, -1]], axis=1)
    padded_global = jnp.pad(everywhere, ((0, 0), (0, per_dev - G), (0, 0), (0, 0))) * (
        device == 0
    ).astype(jnp.float32)
    totals = totals + padded_global
    collected = jnp.einsum(
        "dcb,dcsxf->sbxf",
        chooser.astype(jnp.bfloat16),
        arrived.reshape(seq_count, capacity, 2, BLOCK, features),
        preferred_element_type=jnp.float32,
    )
    totals = totals + collected
    return query_grads.reshape(tokens, features), totals, rim_terms, hold


def on_device(query, key, value, grad_out, rand_blocks):
    kv_stacked = jnp.stack([key, value])
    kv_stacked = lax.all_to_all(kv_stacked, "head", split_axis=2, concat_axis=1, tiled=True)
    keys, values = kv_stacked[0], kv_stacked[1]
    qo_stacked = jnp.stack([query, grad_out])
    qo_stacked = lax.all_to_all(qo_stacked, "head", split_axis=2, concat_axis=1, tiled=True)
    queries, out_grads = qo_stacked[0], qo_stacked[1]
    tokens, features = queries.shape
    head_count = features // HD
    per_dev = tokens // BLOCK
    seq_count = lax.axis_size("seq")
    device = lax.axis_index("seq")
    capacity = (per_dev * R + seq_count - 3) // (seq_count - 2)
    rand_count = per_dev * R
    score_scale = HD ** (-0.5)
    requested = rand_blocks.reshape(seq_count, rand_count)
    owners_all, within_all, rank_all, usable_all = jax.vmap(
        lambda sender: request_plan(requested, sender, per_dev)
    )(jnp.arange(seq_count, dtype=jnp.int32))
    to_me = usable_all & (owners_all == device)
    slot_ids = jnp.arange(capacity)
    block_ids = jnp.arange(per_dev)
    matches = (
        to_me[:, :, None, None]
        & (rank_all[:, :, None, None] == slot_ids[None, None, :, None])
        & (within_all[:, :, None, None] == block_ids[None, None, None, :])
    )
    chooser = jnp.sum(matches.astype(jnp.float32), axis=1)
    my_owners, my_within, my_rank, my_usable = request_plan(requested, device, per_dev)
    my_slot = jnp.clip(my_owners, 0, seq_count - 1) * capacity + my_rank
    own_pairs = jnp.stack([keys, values]).reshape(2, per_dev, BLOCK, features)
    served = jnp.einsum(
        "dcb,sbxf->dcsxf",
        chooser.astype(jnp.bfloat16),
        own_pairs,
        preferred_element_type=jnp.float32,
    ).astype(jnp.bfloat16)
    outgoing = served.reshape(seq_count * capacity, 2, BLOCK, features)
    leading = jnp.stack([keys[: G * BLOCK], values[: G * BLOCK]])
    global_pairs = broadcast(leading, "seq", 0).reshape(2, G, BLOCK, features)
    extended = extended_2(jnp.stack([keys, values]), (("seq", 1),), BLOCK)
    outgoing, global_pairs, extended = lax.optimization_barrier((outgoing, global_pairs, extended))
    chunk_heads = 2 if head_count % 2 == 0 else 1
    chunk_width = chunk_heads * HD
    states = [
        local_chunk(
            queries[:, c0 : c0 + chunk_width],
            out_grads[:, c0 : c0 + chunk_width],
            own_pairs[..., c0 : c0 + chunk_width],
            global_pairs[..., c0 : c0 + chunk_width],
            extended[..., c0 : c0 + chunk_width],
            device,
            seq_count,
        )
        for c0 in range(0, features, chunk_width)
    ]
    pieces = []
    held = ()
    for index, c0 in enumerate(range(0, features, chunk_width)):
        state = states[index] if index == 0 else held[index - 1]
        piece = attend_chunk(
            queries[:, c0 : c0 + chunk_width],
            outgoing[..., c0 : c0 + chunk_width],
            state, chooser, my_slot, my_usable, device, seq_count, capacity,
            hold=tuple(states[1:]) if index == 0 else (),
        )
        if index == 0:
            held = piece[3]
        pieces.append(piece)
    query_grads = jnp.concatenate([p[0] for p in pieces], axis=-1)
    totals = jnp.concatenate([p[1] for p in pieces], axis=-1)
    rim_terms = jnp.concatenate([p[2] for p in pieces], axis=-1)
    rim_terms, totals = lax.optimization_barrier((rim_terms, totals))
    widened = extended_2(rim_terms.astype(jnp.bfloat16), (("seq", 1),), BLOCK).astype(
        rim_terms.dtype
    )
    edges = jnp.concatenate(
        [
            widened[:, None, :BLOCK],
            jnp.zeros((2, per_dev - 2, BLOCK, features), widened.dtype),
            widened[:, None, -BLOCK:],
        ],
        axis=1,
    )
    totals = totals + edges
    grad_rows = query_grads.reshape(tokens, features).astype(jnp.bfloat16)
    key_rows = totals[0].reshape(tokens, features).astype(jnp.bfloat16)
    value_rows = totals[1].reshape(tokens, features).astype(jnp.bfloat16)
    result = jnp.stack([grad_rows, key_rows, value_rows])
    result = lax.all_to_all(result, "head", split_axis=1, concat_axis=2, tiled=True)
    return (result[0], result[1], result[2])


def solution(mesh):
    in_specs = (
        P(("seq", "head"), None),
        P(("seq", "head"), None),
        P(("seq", "head"), None),
        P(("seq", "head"), None),
        P(),
    )
    out_specs = (P(("seq", "head"), None), P(("seq", "head"), None), P(("seq", "head"), None))
    return jax.shard_map(
        on_device, mesh=mesh, in_specs=in_specs, out_specs=out_specs, check_vma=False
    )
```
